1024 devices in a mesh: seq: 64 (over y, x), head: 16 (over z, core).
Axes of the slice: x: 8, y: 8, z: 8, core: 2. Of those that a mesh axis runs over, the one named last changes fastest.
Arguments:
- queries: bfloat16 [8192, 8192], P('seq', 'head'), may hold values from -6 to 6, as said below
- keys: bfloat16 [8192, 1024], P('seq'), may hold values from -6 to 6, as said below
- values: bfloat16 [8192, 1024], P('seq'), may hold values from -6 to 6
- residual: bfloat16 [8192, 8192], P('seq', 'head'), may hold values from -50 to 50
- norm_gain: float32 [8192], replicated, may hold values from 0.25 to 1.75
- block_pos: int32 [1, 64], replicated, may hold values from 0 to 63, each once within a row
- doc_offset: int32 [1, 64], replicated, may hold values from 1 to 128, as said below
Outputs:
- attn_out: bfloat16 [8192, 8192], P('seq', 'head')
- r_factor: float32 [64, 128, 128], P('head')
- whitened: float32 [8192, 8192], P('seq', 'head')
The draws below stay inside these ranges and needn't reach their ends.
Inputs may be any that keep to these rules, and one draw needn't show every extreme that they name: queries may hold rows of large entries. keys may hold rows of large entries. `block_pos`: in each sequence every sequence block is stored exactly once. A document begins at token doc_offset[c, b] of sequence block b when that value is under 128; the first document begins at position 0.
All inputs are finite; a program needn't handle non-finite values.
Results may differ from the reference program's by a relative error of at most 0.0045.
Values may be sent and summed in bfloat16 or wider, within the bound.
No kernel may reach another device: no remote copies, remote signals or barrier semaphores. Data moves between devices by JAX's collectives and lax.ppermute only.
A program may use at most 32 MiB of HBM per device.

```python
import math
import jax
import jax.numpy as jnp
from jax import lax

HEADS = 64
KVH = 8
HD = 128
BLOCK = 128
COPIES = 1
TOKENS = 8192
NBLK = 64
WIDTH = 8192


def draw_queries(key, part):
    sample_key = jax.random.fold_in(key, 1)
    columns = COPIES * HEADS * HD
    result = jnp.clip(jax.random.normal(sample_key, (TOKENS, columns), jnp.float32), -6.0, 6.0)
    return result.astype(jnp.bfloat16)


def draw_keys(key, part):
    sample_key = jax.random.fold_in(key, 2)
    columns = COPIES * KVH * HD
    result = jnp.clip(jax.random.normal(sample_key, (TOKENS, columns), jnp.float32), -6.0, 6.0)
    return result.astype(jnp.bfloat16)


def draw_residual(key, part):
    columns = COPIES * WIDTH
    row_scale = jnp.exp(jax.random.uniform(jax.random.fold_in(key, 31), (TOKENS,), jnp.float32, math.log(0.1), 0.0))
    place = (jnp.arange(columns, dtype=jnp.int32) % WIDTH).astype(jnp.float32)
    column_rise = jnp.exp(math.log(10.0) * place / (WIDTH - 1))
    column_jitter = jnp.exp(jax.random.uniform(jax.random.fold_in(key, 32), (columns,), jnp.float32, -0.5, 0.5))
    sample_key = jax.random.fold_in(key, 33)
    base = jax.random.normal(sample_key, (TOKENS, columns), jnp.float32)
    base = jnp.clip(base, -6.0, 6.0)
    return (0.5 * base * row_scale[:, None] * (column_rise * column_jitter)[None, :]).astype(jnp.bfloat16)


def draw_doc_offset(key, part):
    starting = jax.random.randint(jax.random.fold_in(key, 21), (COPIES, NBLK), 0, 8) == 0
    placed = jax.random.randint(jax.random.fold_in(key, 22), (COPIES, NBLK), 1, BLOCK)
    result = jnp.where(starting, placed, BLOCK)
    result = result.at[:, 0].set(BLOCK)
    return result.astype(jnp.int32)


def level_of(own_key, shape, cuts, smallest, top_value):
    loudness = 1.0
    for position, parts in cuts:
        steps = jax.random.uniform(jax.random.fold_in(jax.random.fold_in(own_key, 6), position), (parts,), jnp.float32, smallest / len(cuts), top_value / len(cuts))
        loudness = loudness * jnp.repeat(jnp.exp(steps), shape[position] // parts).reshape((-1,) + (1,) * (len(shape) - 1 - position))
    return loudness


def centred(key, dims, deviation, most, split=(), kind=jnp.bfloat16):
    entries = jax.random.normal(key, dims, jnp.float32) * deviation
    if len(split) > 0:
        entries = level_of(key, dims, split, -0.22, 0.18) * entries
    return jnp.clip(entries, min=-most, max=most).astype(kind)


def setup_inputs(seed: int = 0) -> dict:
    splits = jax.random.split(jax.random.key(seed), 8)
    return {
        "queries": draw_queries(jax.random.fold_in(splits[7], 71), 0),
        "keys": draw_keys(jax.random.fold_in(splits[7], 71), 0),
        "values": centred(splits[2], (TOKENS, COPIES * KVH * HD), 1.0, 6.0, ((0, 64),)),
        "residual": draw_residual(jax.random.fold_in(splits[7], 71), 0),
        "norm_gain": jnp.clip(1.0 + 0.15 * jax.random.normal(splits[4], (WIDTH,), jnp.float32), 0.25, 1.75),
        "block_pos": jax.vmap(lambda own: jax.random.permutation(own, NBLK))(jax.random.split(splits[5], COPIES)).reshape((COPIES, NBLK)).astype(jnp.int32),
        "doc_offset": draw_doc_offset(jax.random.fold_in(splits[7], 71), 0),
    }


EPSILON = 1e-05

def positions_and_docs(block_pos, doc_offset):
    block_total = block_pos.shape[0]
    doc_flags = (doc_offset < BLOCK).astype(jnp.int32)
    starts_before = (jnp.cumsum(doc_flags) - doc_flags).astype(jnp.int32)
    matches = block_pos[:, None] == jnp.arange(block_total, dtype=jnp.int32)[None, :]
    start_count = lax.optimization_barrier(jnp.sum(jnp.where(matches, starts_before[None, :], 0), axis=1)).astype(jnp.int32)
    offsets = lax.optimization_barrier(jnp.sum(jnp.where(matches, doc_offset[None, :], 0), axis=1)).astype(jnp.int32)
    within = jnp.arange(BLOCK, dtype=jnp.int32)
    seq_pos = (block_pos[:, None] * BLOCK + within[None, :]).reshape(-1).astype(jnp.int32)
    doc_id = (start_count[:, None] + (within[None, :] >= offsets[:, None]).astype(jnp.int32)).reshape(-1)
    return (seq_pos, doc_id.astype(jnp.int32))

def one_sequence(queries, keys, values, residual, norm_gain, block_pos, doc_offset):
    seq_pos, doc_id = positions_and_docs(block_pos, doc_offset)
    visible = (seq_pos[None, :] <= seq_pos[:, None]) & (doc_id[None, :] == doc_id[:, None])
    group_size = HEADS // KVH
    score_scale = 1.0 / math.sqrt(HD)

    def one_head(head_index):
        query_cols = lax.dynamic_slice_in_dim(queries, head_index * HD, HD, 1)
        share = head_index // group_size
        key_cols = lax.dynamic_slice_in_dim(keys, share * HD, HD, 1)
        value_cols = lax.dynamic_slice_in_dim(values, share * HD, HD, 1)
        scores = jnp.dot(query_cols.astype(jnp.float32), key_cols.T.astype(jnp.float32), preferred_element_type=jnp.float32) * score_scale
        scores = jnp.where(visible, scores, -jnp.inf)
        row_max = lax.optimization_barrier(jnp.max(scores, axis=1, keepdims=True))
        expo = jnp.exp(scores - row_max)
        totals = lax.optimization_barrier(jnp.sum(expo, axis=1, keepdims=True))
        output = jnp.dot(expo.astype(jnp.bfloat16).astype(jnp.float32), value_cols.astype(jnp.float32), preferred_element_type=jnp.float32) / totals
        return output.astype(jnp.bfloat16)
    per_head = lax.map(one_head, jnp.arange(HEADS, dtype=jnp.int32))
    attn_out = jnp.transpose(per_head, (1, 0, 2)).reshape(TOKENS, WIDTH)
    mixed = attn_out.astype(jnp.float32) + residual.astype(jnp.float32)
    square_sum = lax.optimization_barrier(jnp.sum(mixed * mixed, axis=1, keepdims=True))
    normed = mixed * lax.rsqrt(square_sum / WIDTH + EPSILON) * norm_gain[None, :]
    blocks = normed.reshape(TOKENS, HEADS, HD)
    gram_sum = jnp.einsum('rhc,rhd->hcd', blocks, blocks, precision=lax.Precision.HIGHEST)
    lower_factor = jnp.linalg.cholesky(gram_sum)
    r_factor = jnp.transpose(lower_factor, (0, 2, 1)) / math.sqrt(TOKENS)
    solved = jax.scipy.linalg.solve_triangular(lower_factor, jnp.transpose(blocks, (1, 2, 0)), lower=True)
    whitened = jnp.transpose(solved, (2, 0, 1)).reshape(TOKENS, WIDTH) * math.sqrt(TOKENS)
    return (attn_out, r_factor, whitened)

def reference(queries, keys, values, residual, norm_gain, block_pos, doc_offset):
    outputs = []
    factors = []
    whites = []
    kv_width = KVH * HD
    for copy in range(COPIES):
        attn_part, factor_part, white_part = one_sequence(queries[:, copy * WIDTH:(copy + 1) * WIDTH], keys[:, copy * kv_width:(copy + 1) * kv_width], values[:, copy * kv_width:(copy + 1) * kv_width], residual[:, copy * WIDTH:(copy + 1) * WIDTH], norm_gain, block_pos[copy], doc_offset[copy])
        outputs.append(attn_part)
        factors.append(factor_part)
        whites.append(white_part)
    return (jnp.concatenate(outputs, axis=1), jnp.concatenate(factors, axis=0), jnp.concatenate(whites, axis=1))
```

```python
import math

import jax
import jax.numpy as jnp
from jax import lax
from jax.sharding import PartitionSpec as P

HEADS = 64
KVH = 8
HD = 128
BLOCK = 128
COPIES = 1
WIDTH = 8192


EPSILON = 1e-05


def side_by_side(arrays, axis, dim, along):
    both = jnp.concatenate(arrays, axis=along)
    whole, at, done = (lax.all_gather(both, axis, axis=dim, tiled=True), 0, [])
    for a in arrays:
        done.append(lax.slice_in_dim(whole, at, at + a.shape[along], axis=along))
        at += a.shape[along]
    return tuple(done)


def copy_for_each(shard, axis):
    count = lax.axis_size(axis)
    return lax.all_to_all(
        jnp.broadcast_to(shard[None], (count, *shard.shape)), axis, 0, 0, tiled=True
    )


def over_copies(shard, axis):
    everything = copy_for_each(shard, axis)
    return jnp.sum(everything, axis=0)


def positions_and_docs(block_pos, doc_offset):
    block_total = block_pos.shape[0]
    doc_flags = (doc_offset < BLOCK).astype(jnp.int32)
    starts_before = jnp.cumsum(doc_flags) - doc_flags
    matches = block_pos[:, None] == jnp.arange(block_total, dtype=jnp.int32)[None, :]
    start_count = jnp.sum(jnp.where(matches, starts_before[None, :], 0), axis=1)
    offsets = jnp.sum(jnp.where(matches, doc_offset[None, :], 0), axis=1)
    within = jnp.arange(BLOCK, dtype=jnp.int32)
    seq_pos = (block_pos[:, None] * BLOCK + within[None, :]).reshape(-1)
    doc_id = (
        start_count[:, None] + (within[None, :] >= offsets[:, None]).astype(jnp.int32)
    ).reshape(-1)
    return (seq_pos, doc_id)


def gram_of(matrix):
    return jnp.einsum("hnc,hnd->hcd", matrix, matrix, precision=lax.Precision.HIGHEST)


SEQ = ("y", "x")
HEAD = ("z", "c")


def local(queries, keys, values, residual, norm_gain, block_pos, doc_offset):
    row_count = queries.shape[0]
    head_count = queries.shape[1] // HD
    group_size = HEADS // KVH
    share_count = max(1, head_count // group_size)
    per_share = head_count // share_count
    total_rows = row_count * lax.axis_size(SEQ)
    global_first = lax.axis_index(HEAD) * head_count
    copy_index = global_first // HEADS
    first_head = global_first % HEADS
    first_share = first_head // group_size
    key_start = copy_index * (KVH * HD) + first_share * HD
    key_cols = lax.dynamic_slice_in_dim(keys, key_start, share_count * HD, 1)
    value_cols = lax.dynamic_slice_in_dim(values, key_start, share_count * HD, 1)
    own_blocks = lax.dynamic_index_in_dim(block_pos, copy_index, 0, keepdims=False)
    own_offsets = lax.dynamic_index_in_dim(doc_offset, copy_index, 0, keepdims=False)
    gain_cols = lax.dynamic_slice_in_dim(norm_gain, first_head * HD, head_count * HD)
    seq_pos, doc_id = positions_and_docs(own_blocks, own_offsets)
    first_row = lax.axis_index(SEQ) * row_count
    own_pos = lax.dynamic_slice_in_dim(seq_pos, first_row, row_count)
    own_doc = lax.dynamic_slice_in_dim(doc_id, first_row, row_count)
    query_heads = queries.reshape(row_count, share_count, per_share, HD)
    score_scale = 1.0 / math.sqrt(HD)

    def attend_block(state_now, key_piece, value_piece, first_key):
        length = key_piece.shape[0]
        key_pos = lax.dynamic_slice_in_dim(seq_pos, first_key, length)
        key_doc = lax.dynamic_slice_in_dim(doc_id, first_key, length)
        seen = (key_pos[None, :] <= own_pos[:, None]) & (key_doc[None, :] == own_doc[:, None])

        def accumulate(state_inner):
            run_max, run_total, run_acc = state_inner
            key_heads = key_piece.reshape(length, share_count, HD)
            value_heads = value_piece.reshape(length, share_count, HD)
            scores = (
                jnp.einsum(
                    "rkgd,nkd->kgrn", query_heads, key_heads, preferred_element_type=jnp.float32
                )
                * score_scale
            )
            scores = jnp.where(seen[None, None], scores, -jnp.inf)
            new_max = jnp.maximum(run_max, jnp.max(scores, axis=3))
            factor = jnp.exp(run_max - new_max)
            expo = jnp.exp(scores - new_max[..., None])
            new_total = run_total * factor + jnp.sum(expo, axis=3)
            partial_value = jnp.einsum(
                "kgrn,nkd->kgrd",
                expo.astype(jnp.bfloat16),
                value_heads,
                preferred_element_type=jnp.float32,
            )
            new_acc = run_acc * factor[..., None] + partial_value
            return (new_max, new_total, new_acc)

        def unchanged(state_inner):
            return state_inner

        return lax.cond(jnp.any(seen), accumulate, unchanged, state_now)

    start_state = (
        jnp.full((share_count, per_share, row_count), -1e30, jnp.float32),
        jnp.zeros((share_count, per_share, row_count), jnp.float32),
        jnp.zeros((share_count, per_share, row_count, HD), jnp.float32),
    )
    core = lax.axis_index("c")
    mine = jnp.where(core == 0, key_cols, value_cols)
    gathered = lax.all_gather(lax.all_gather(mine, "x", axis=0, tiled=True), "y", axis=0, tiled=True)
    other = lax.ppermute(gathered, "c", perm=[(0, 1), (1, 0)])
    key_piece = jnp.where(core == 0, gathered, other)
    value_piece = jnp.where(core == 0, other, gathered)
    length = key_piece.shape[0]
    step_rows = math.gcd(length, 1024)

    def advance(step_index, state_inner):
        begin_row = step_index * step_rows
        key_part = lax.dynamic_slice_in_dim(key_piece, begin_row, step_rows, 0)
        value_part = lax.dynamic_slice_in_dim(value_piece, begin_row, step_rows, 0)
        return attend_block(state_inner, key_part, value_part, begin_row)

    final_max, final_total, final_acc = lax.fori_loop(0, length // step_rows, advance, start_state)
    output = final_acc / final_total[..., None]
    attn_out = (
        jnp.transpose(output, (2, 0, 1, 3)).reshape(row_count, head_count * HD).astype(jnp.bfloat16)
    )
    mixed = attn_out.astype(jnp.float32) + residual.astype(jnp.float32)
    local_squares = jnp.sum(mixed * mixed, axis=1)
    slot_mask = jnp.arange(COPIES, dtype=jnp.int32) == copy_index
    slotted = jnp.where(slot_mask[:, None], local_squares[None, :], 0.0)
    summed = over_copies(slotted, HEAD)
    square_sum = lax.dynamic_index_in_dim(summed, copy_index, 0, keepdims=False)
    normed = mixed * lax.rsqrt(square_sum[:, None] / WIDTH + EPSILON) * gain_cols[None, :]
    blocks = normed.reshape(row_count, head_count, HD)
    head_rows = jnp.transpose(blocks, (1, 0, 2))
    gram_sum = lax.psum(lax.optimization_barrier(lax.psum(gram_of(head_rows), "x")), "y")
    lower_factor = jnp.linalg.cholesky(gram_sum)
    r_factor = jnp.transpose(lower_factor, (0, 2, 1)) / math.sqrt(total_rows)
    solved = jax.scipy.linalg.solve_triangular(
        lower_factor, jnp.transpose(blocks, (1, 2, 0)), lower=True
    )
    whitened = jnp.transpose(solved, (2, 0, 1)).reshape(row_count, head_count * HD) * math.sqrt(
        total_rows
    )
    return (attn_out, r_factor, whitened)


def solution(mesh):
    seq_size, head_size = mesh.devices.shape
    side = math.isqrt(seq_size)
    grid = jax.sharding.Mesh(
        mesh.devices.reshape(side, seq_size // side, head_size // 2, 2), ("y", "x", "z", "c")
    )
    return jax.shard_map(
        local,
        mesh=grid,
        in_specs=(
            P(SEQ, HEAD),
            P(SEQ, None),
            P(SEQ, None),
            P(SEQ, HEAD),
            P(),
            P(),
            P(),
        ),
        out_specs=(P(SEQ, HEAD), P(HEAD, None, None), P(SEQ, HEAD)),
        check_vma=False,
    )
```

```python
import math

import jax
import jax.numpy as jnp
from jax import lax
from jax.sharding import PartitionSpec as P

HEADS = 64
KVH = 8
HD = 128
BLOCK = 128
COPIES = 1
WIDTH = 8192


EPSILON = 1e-05


def side_by_side(arrays, axis, dim, along):
    both = jnp.concatenate(arrays, axis=along)
    whole, at, done = (lax.all_gather(both, axis, axis=dim, tiled=True), 0, [])
    for a in arrays:
        done.append(lax.slice_in_dim(whole, at, at + a.shape[along], axis=along))
        at += a.shape[along]
    return tuple(done)


def copy_for_each(shard, axis):
    count = lax.axis_size(axis)
    return lax.all_to_all(
        jnp.broadcast_to(shard[None], (count, *shard.shape)), axis, 0, 0, tiled=True
    )


def over_copies(shard, axis):
    everything = copy_for_each(shard, axis)
    return jnp.sum(everything, axis=0)


def exchange_sum(value, axis):
    count = lax.axis_size(axis)
    step = 1
    while step < count:
        partner = lax.ppermute(value, axis, [(i, i ^ step) for i in range(count)])
        value = value + partner
        step *= 2
    return value


def exchange_gather(value, axis):
    count = lax.axis_size(axis)
    me = lax.axis_index(axis)
    step = 1
    while step < count:
        partner = lax.ppermute(value, axis, [(i, i ^ step) for i in range(count)])
        low = (me & step) == 0
        first = jnp.where(low, value, partner)
        second = jnp.where(low, partner, value)
        value = jnp.concatenate([first, second], axis=0)
        step *= 2
    return value


def positions_and_docs(block_pos, doc_offset):
    block_total = block_pos.shape[0]
    doc_flags = (doc_offset < BLOCK).astype(jnp.int32)
    starts_before = jnp.cumsum(doc_flags) - doc_flags
    matches = block_pos[:, None] == jnp.arange(block_total, dtype=jnp.int32)[None, :]
    start_count = jnp.sum(jnp.where(matches, starts_before[None, :], 0), axis=1)
    offsets = jnp.sum(jnp.where(matches, doc_offset[None, :], 0), axis=1)
    within = jnp.arange(BLOCK, dtype=jnp.int32)
    seq_pos = (block_pos[:, None] * BLOCK + within[None, :]).reshape(-1)
    doc_id = (
        start_count[:, None] + (within[None, :] >= offsets[:, None]).astype(jnp.int32)
    ).reshape(-1)
    return (seq_pos, doc_id)


def gram_of(matrix):
    return jnp.einsum("hnc,hnd->hcd", matrix, matrix, precision=lax.Precision.HIGHEST)


SEQ = ("y", "x")
HEAD = ("z", "c")


def local(queries, keys, values, residual, norm_gain, block_pos, doc_offset):
    row_count = queries.shape[0]
    head_count = queries.shape[1] // HD
    group_size = HEADS // KVH
    share_count = max(1, head_count // group_size)
    per_share = head_count // share_count
    total_rows = row_count * lax.axis_size(SEQ)
    global_first = lax.axis_index(HEAD) * head_count
    copy_index = global_first // HEADS
    first_head = global_first % HEADS
    first_share = first_head // group_size
    key_start = copy_index * (KVH * HD) + first_share * HD
    key_cols = lax.dynamic_slice_in_dim(keys, key_start, share_count * HD, 1)
    value_cols = lax.dynamic_slice_in_dim(values, key_start, share_count * HD, 1)
    own_blocks = lax.dynamic_index_in_dim(block_pos, copy_index, 0, keepdims=False)
    own_offsets = lax.dynamic_index_in_dim(doc_offset, copy_index, 0, keepdims=False)
    gain_cols = lax.dynamic_slice_in_dim(norm_gain, first_head * HD, head_count * HD)
    seq_pos, doc_id = positions_and_docs(own_blocks, own_offsets)
    first_row = lax.axis_index(SEQ) * row_count
    own_pos = lax.dynamic_slice_in_dim(seq_pos, first_row, row_count)
    own_doc = lax.dynamic_slice_in_dim(doc_id, first_row, row_count)
    query_heads = queries.reshape(row_count, share_count, per_share, HD)
    score_scale = 1.0 / math.sqrt(HD)

    def attend_block(state_now, key_piece, value_piece, first_key):
        length = key_piece.shape[0]
        key_pos = lax.dynamic_slice_in_dim(seq_pos, first_key, length)
        key_doc = lax.dynamic_slice_in_dim(doc_id, first_key, length)
        seen = (key_pos[None, :] <= own_pos[:, None]) & (key_doc[None, :] == own_doc[:, None])

        def accumulate(state_inner):
            run_max, run_total, run_acc = state_inner
            key_heads = key_piece.reshape(length, share_count, HD)
            value_heads = value_piece.reshape(length, share_count, HD)
            scores = (
                jnp.einsum(
                    "rkgd,nkd->kgrn", query_heads, key_heads, preferred_element_type=jnp.float32
                )
                * score_scale
            )
            scores = jnp.where(seen[None, None], scores, -jnp.inf)
            new_max = jnp.maximum(run_max, jnp.max(scores, axis=3))
            factor = jnp.exp(run_max - new_max)
            expo = jnp.exp(scores - new_max[..., None])
            new_total = run_total * factor + jnp.sum(expo, axis=3)
            partial_value = jnp.einsum(
                "kgrn,nkd->kgrd",
                expo.astype(jnp.bfloat16),
                value_heads,
                preferred_element_type=jnp.float32,
            )
            new_acc = run_acc * factor[..., None] + partial_value
            return (new_max, new_total, new_acc)

        def unchanged(state_inner):
            return state_inner

        return lax.cond(jnp.any(seen), accumulate, unchanged, state_now)

    start_state = (
        jnp.full((share_count, per_share, row_count), -1e30, jnp.float32),
        jnp.zeros((share_count, per_share, row_count), jnp.float32),
        jnp.zeros((share_count, per_share, row_count, HD), jnp.float32),
    )
    core = lax.axis_index("c")
    mine = jnp.where(core == 0, key_cols, value_cols)
    gathered = lax.all_gather(exchange_gather(mine, "x"), "y", axis=0, tiled=True)
    other = lax.ppermute(gathered, "c", perm=[(0, 1), (1, 0)])
    key_piece = jnp.where(core == 0, gathered, other)
    value_piece = jnp.where(core == 0, other, gathered)
    length = key_piece.shape[0]
    step_rows = math.gcd(length, 1024)

    def advance(step_index, state_inner):
        begin_row = step_index * step_rows
        key_part = lax.dynamic_slice_in_dim(key_piece, begin_row, step_rows, 0)
        value_part = lax.dynamic_slice_in_dim(value_piece, begin_row, step_rows, 0)
        return attend_block(state_inner, key_part, value_part, begin_row)

    final_max, final_total, final_acc = lax.fori_loop(0, length // step_rows, advance, start_state)
    output = final_acc / final_total[..., None]
    attn_out = (
        jnp.transpose(output, (2, 0, 1, 3)).reshape(row_count, head_count * HD).astype(jnp.bfloat16)
    )
    mixed = attn_out.astype(jnp.float32) + residual.astype(jnp.float32)
    local_squares = jnp.sum(mixed * mixed, axis=1)
    slot_mask = jnp.arange(COPIES, dtype=jnp.int32) == copy_index
    slotted = jnp.where(slot_mask[:, None], local_squares[None, :], 0.0)
    summed = over_copies(slotted, HEAD)
    square_sum = lax.dynamic_index_in_dim(summed, copy_index, 0, keepdims=False)
    normed = mixed * lax.rsqrt(square_sum[:, None] / WIDTH + EPSILON) * gain_cols[None, :]
    blocks = normed.reshape(row_count, head_count, HD)
    head_rows = jnp.transpose(blocks, (1, 0, 2))
    gram_sum = exchange_sum(exchange_sum(gram_of(head_rows), "x"), "y")
    lower_factor = jnp.linalg.cholesky(gram_sum)
    r_factor = jnp.transpose(lower_factor, (0, 2, 1)) / math.sqrt(total_rows)
    solved = jax.scipy.linalg.solve_triangular(
        lower_factor, jnp.transpose(blocks, (1, 2, 0)), lower=True
    )
    whitened = jnp.transpose(solved, (2, 0, 1)).reshape(row_count, head_count * HD) * math.sqrt(
        total_rows
    )
    return (attn_out, r_factor, whitened)


def solution(mesh):
    seq_size, head_size = mesh.devices.shape
    side = math.isqrt(seq_size)
    grid = jax.sharding.Mesh(
        mesh.devices.reshape(side, seq_size // side, head_size // 2, 2), ("y", "x", "z", "c")
    )
    return jax.shard_map(
        local,
        mesh=grid,
        in_specs=(
            P(SEQ, HEAD),
            P(SEQ, None),
            P(SEQ, None),
            P(SEQ, HEAD),
            P(),
            P(),
            P(),
        ),
        out_specs=(P(SEQ, HEAD), P(HEAD, None, None), P(SEQ, HEAD)),
        check_vma=False,
    )
```

```python
import math

import jax
import jax.numpy as jnp
from jax import lax
from jax.experimental import pallas as pl
from jax.experimental.pallas import tpu as pltpu
from jax.sharding import PartitionSpec as P

HEADS = 64
KVH = 8
HD = 128
BLOCK = 128
COPIES = 1
WIDTH = 8192


EPSILON = 1e-05


def side_by_side(arrays, axis, dim, along):
    both = jnp.concatenate(arrays, axis=along)
    whole, at, done = (lax.all_gather(both, axis, axis=dim, tiled=True), 0, [])
    for a in arrays:
        done.append(lax.slice_in_dim(whole, at, at + a.shape[along], axis=along))
        at += a.shape[along]
    return tuple(done)


def copy_for_each(shard, axis):
    count = lax.axis_size(axis)
    return lax.all_to_all(
        jnp.broadcast_to(shard[None], (count, *shard.shape)), axis, 0, 0, tiled=True
    )


def over_copies(shard, axis):
    everything = copy_for_each(shard, axis)
    return jnp.sum(everything, axis=0)


def factor_kernel(g_ref, u_ref, li_ref, m_ref):
    heads, n, _ = g_ref.shape
    row_ids = lax.broadcasted_iota(jnp.int32, (n, 1), 0)
    lane_ids = lax.broadcasted_iota(jnp.int32, (1, n), 1)
    eye = (lax.broadcasted_iota(jnp.int32, (n, n), 0) == lax.broadcasted_iota(jnp.int32, (n, n), 1)).astype(jnp.float32)
    for h in range(heads):
        m_ref[h, :, :n] = g_ref[h]
        m_ref[h, :, n:] = eye

    def step(j, carry):
        pick = lane_ids == j
        for h in range(heads):
            row = m_ref[h, pl.ds(j, 1), :]
            pivot = jnp.sum(jnp.where(pick, row[:, :n], 0.0), axis=1, keepdims=True)
            scale = lax.rsqrt(pivot)
            scaled = row * scale
            column = jnp.sum(jnp.where(pick, m_ref[h, :, :n], 0.0), axis=1, keepdims=True)
            column = jnp.where(row_ids > j, column * scale, 0.0)
            m_ref[h] = m_ref[h] - column * scaled
            m_ref[h, pl.ds(j, 1), :] = scaled
        return carry

    lax.fori_loop(0, n, step, 0)
    upper = lax.broadcasted_iota(jnp.int32, (n, n), 0) <= lax.broadcasted_iota(jnp.int32, (n, n), 1)
    for h in range(heads):
        u_ref[h] = jnp.where(upper, m_ref[h, :, :n], 0.0)
        li_ref[h] = m_ref[h, :, n:]


def factor(gram):
    heads, n, _ = gram.shape
    shape = jax.ShapeDtypeStruct((heads, n, n), jnp.float32)
    return pl.pallas_call(
        factor_kernel,
        out_shape=(shape, shape),
        in_specs=[pl.BlockSpec(memory_space=pltpu.VMEM)],
        out_specs=(pl.BlockSpec(memory_space=pltpu.VMEM), pl.BlockSpec(memory_space=pltpu.VMEM)),
        scratch_shapes=[pltpu.VMEM((heads, n, 2 * n), jnp.float32)],
    )(gram)


def exchange_sum(value, axis):
    count = lax.axis_size(axis)
    step = 1
    while step < count:
        partner = lax.ppermute(value, axis, [(i, i ^ step) for i in range(count)])
        value = value + partner
        step *= 2
    return value


def exchange_gather(value, axis):
    count = lax.axis_size(axis)
    me = lax.axis_index(axis)
    step = 1
    while step < count:
        partner = lax.ppermute(value, axis, [(i, i ^ step) for i in range(count)])
        low = (me & step) == 0
        first = jnp.where(low, value, partner)
        second = jnp.where(low, partner, value)
        value = jnp.concatenate([first, second], axis=0)
        step *= 2
    return value


def positions_and_docs(block_pos, doc_offset):
    block_total = block_pos.shape[0]
    doc_flags = (doc_offset < BLOCK).astype(jnp.int32)
    starts_before = jnp.cumsum(doc_flags) - doc_flags
    matches = block_pos[:, None] == jnp.arange(block_total, dtype=jnp.int32)[None, :]
    start_count = jnp.sum(jnp.where(matches, starts_before[None, :], 0), axis=1)
    offsets = jnp.sum(jnp.where(matches, doc_offset[None, :], 0), axis=1)
    within = jnp.arange(BLOCK, dtype=jnp.int32)
    seq_pos = (block_pos[:, None] * BLOCK + within[None, :]).reshape(-1)
    doc_id = (
        start_count[:, None] + (within[None, :] >= offsets[:, None]).astype(jnp.int32)
    ).reshape(-1)
    return (seq_pos, doc_id)


def gram_of(matrix):
    return jnp.einsum("hnc,hnd->hcd", matrix, matrix, precision=lax.Precision.HIGHEST)


SEQ = ("y", "x")
HEAD = ("z", "c")


def local(queries, keys, values, residual, norm_gain, block_pos, doc_offset):
    row_count = queries.shape[0]
    head_count = queries.shape[1] // HD
    group_size = HEADS // KVH
    share_count = max(1, head_count // group_size)
    per_share = head_count // share_count
    total_rows = row_count * lax.axis_size(SEQ)
    global_first = lax.axis_index(HEAD) * head_count
    copy_index = global_first // HEADS
    first_head = global_first % HEADS
    first_share = first_head // group_size
    key_start = copy_index * (KVH * HD) + first_share * HD
    key_cols = lax.dynamic_slice_in_dim(keys, key_start, share_count * HD, 1)
    value_cols = lax.dynamic_slice_in_dim(values, key_start, share_count * HD, 1)
    own_blocks = lax.dynamic_index_in_dim(block_pos, copy_index, 0, keepdims=False)
    own_offsets = lax.dynamic_index_in_dim(doc_offset, copy_index, 0, keepdims=False)
    gain_cols = lax.dynamic_slice_in_dim(norm_gain, first_head * HD, head_count * HD)
    seq_pos, doc_id = positions_and_docs(own_blocks, own_offsets)
    first_row = lax.axis_index(SEQ) * row_count
    own_pos = lax.dynamic_slice_in_dim(seq_pos, first_row, row_count)
    own_doc = lax.dynamic_slice_in_dim(doc_id, first_row, row_count)
    query_heads = queries.reshape(row_count, share_count, per_share, HD)
    score_scale = 1.0 / math.sqrt(HD)

    def attend_block(state_now, key_piece, value_piece, first_key):
        length = key_piece.shape[0]
        key_pos = lax.dynamic_slice_in_dim(seq_pos, first_key, length)
        key_doc = lax.dynamic_slice_in_dim(doc_id, first_key, length)
        seen = (key_pos[None, :] <= own_pos[:, None]) & (key_doc[None, :] == own_doc[:, None])

        def accumulate(state_inner):
            run_max, run_total, run_acc = state_inner
            key_heads = key_piece.reshape(length, share_count, HD)
            value_heads = value_piece.reshape(length, share_count, HD)
            scores = (
                jnp.einsum(
                    "rkgd,nkd->kgrn", query_heads, key_heads, preferred_element_type=jnp.float32
                )
                * score_scale
            )
            scores = jnp.where(seen[None, None], scores, -jnp.inf)
            new_max = jnp.maximum(run_max, jnp.max(scores, axis=3))
            factor = jnp.exp(run_max - new_max)
            expo = jnp.exp(scores - new_max[..., None])
            new_total = run_total * factor + jnp.sum(expo, axis=3)
            partial_value = jnp.einsum(
                "kgrn,nkd->kgrd",
                expo.astype(jnp.bfloat16),
                value_heads,
                preferred_element_type=jnp.float32,
            )
            new_acc = run_acc * factor[..., None] + partial_value
            return (new_max, new_total, new_acc)

        def unchanged(state_inner):
            return state_inner

        return lax.cond(jnp.any(seen), accumulate, unchanged, state_now)

    start_state = (
        jnp.full((share_count, per_share, row_count), -1e30, jnp.float32),
        jnp.zeros((share_count, per_share, row_count), jnp.float32),
        jnp.zeros((share_count, per_share, row_count, HD), jnp.float32),
    )
    core = lax.axis_index("c")
    mine = jnp.where(core == 0, key_cols, value_cols)
    gathered = lax.all_gather(exchange_gather(mine, "x"), "y", axis=0, tiled=True)
    other = lax.ppermute(gathered, "c", perm=[(0, 1), (1, 0)])
    key_piece = jnp.where(core == 0, gathered, other)
    value_piece = jnp.where(core == 0, other, gathered)
    length = key_piece.shape[0]
    step_rows = math.gcd(length, 1024)

    def advance(step_index, state_inner):
        begin_row = step_index * step_rows
        key_part = lax.dynamic_slice_in_dim(key_piece, begin_row, step_rows, 0)
        value_part = lax.dynamic_slice_in_dim(value_piece, begin_row, step_rows, 0)
        return attend_block(state_inner, key_part, value_part, begin_row)

    final_max, final_total, final_acc = lax.fori_loop(0, length // step_rows, advance, start_state)
    output = final_acc / final_total[..., None]
    attn_out = (
        jnp.transpose(output, (2, 0, 1, 3)).reshape(row_count, head_count * HD).astype(jnp.bfloat16)
    )
    mixed = attn_out.astype(jnp.float32) + residual.astype(jnp.float32)
    local_squares = jnp.sum(mixed * mixed, axis=1)
    slot_mask = jnp.arange(COPIES, dtype=jnp.int32) == copy_index
    slotted = jnp.where(slot_mask[:, None], local_squares[None, :], 0.0)
    summed = over_copies(slotted, HEAD)
    square_sum = lax.dynamic_index_in_dim(summed, copy_index, 0, keepdims=False)
    normed = mixed * lax.rsqrt(square_sum[:, None] / WIDTH + EPSILON) * gain_cols[None, :]
    blocks = normed.reshape(row_count, head_count, HD)
    head_rows = jnp.transpose(blocks, (1, 0, 2))
    gram_sum = exchange_sum(exchange_sum(gram_of(head_rows), "x"), "y")
    upper_factor, lower_inverse = factor(gram_sum)
    r_factor = upper_factor / math.sqrt(total_rows)
    solved = jnp.einsum("rhc,hdc->rhd", blocks, lower_inverse, precision=lax.Precision.HIGHEST)
    whitened = solved.reshape(row_count, head_count * HD) * math.sqrt(total_rows)
    return (attn_out, r_factor, whitened)


def solution(mesh):
    seq_size, head_size = mesh.devices.shape
    side = math.isqrt(seq_size)
    grid = jax.sharding.Mesh(
        mesh.devices.reshape(side, seq_size // side, head_size // 2, 2), ("y", "x", "z", "c")
    )
    return jax.shard_map(
        local,
        mesh=grid,
        in_specs=(
            P(SEQ, HEAD),
            P(SEQ, None),
            P(SEQ, None),
            P(SEQ, HEAD),
            P(),
            P(),
            P(),
        ),
        out_specs=(P(SEQ, HEAD), P(HEAD, None, None), P(SEQ, HEAD)),
        check_vma=False,
    )
```

```python
import math

import jax
import jax.numpy as jnp
from jax import lax
from jax.experimental import pallas as pl
from jax.experimental.pallas import tpu as pltpu
from jax.sharding import PartitionSpec as P

HEADS = 64
KVH = 8
HD = 128
BLOCK = 128
COPIES = 1
WIDTH = 8192


EPSILON = 1e-05


def side_by_side(arrays, axis, dim, along):
    both = jnp.concatenate(arrays, axis=along)
    whole, at, done = (lax.all_gather(both, axis, axis=dim, tiled=True), 0, [])
    for a in arrays:
        done.append(lax.slice_in_dim(whole, at, at + a.shape[along], axis=along))
        at += a.shape[along]
    return tuple(done)


def copy_for_each(shard, axis):
    count = lax.axis_size(axis)
    return lax.all_to_all(
        jnp.broadcast_to(shard[None], (count, *shard.shape)), axis, 0, 0, tiled=True
    )


def over_copies(shard, axis):
    everything = copy_for_each(shard, axis)
    return jnp.sum(everything, axis=0)


TILE = 16


def factor_kernel(g_ref, u_ref, li_ref, m_ref):
    heads, n, _ = g_ref.shape
    lane_ids = lax.broadcasted_iota(jnp.int32, (1, n), 1)
    tile_rows = lax.broadcasted_iota(jnp.int32, (TILE, 1), 0)
    eye = (lax.broadcasted_iota(jnp.int32, (n, n), 0) == lax.broadcasted_iota(jnp.int32, (n, n), 1)).astype(jnp.float32)
    for h in range(heads):
        m_ref[h, :, :n] = g_ref[h]
        m_ref[h, :, n:] = eye

    def step(j, carry):
        pick = lane_ids == j
        scales, rows = [], []
        for h in range(heads):
            row = m_ref[h, pl.ds(j, 1), :]
            pivot = jnp.sum(jnp.where(pick, row[:, :n], 0.0), axis=1, keepdims=True)
            scale = lax.rsqrt(pivot)
            scaled = row * scale
            m_ref[h, pl.ds(j, 1), :] = scaled
            scales.append(scale)
            rows.append(scaled)

        def update(t, inner):
            first = pl.multiple_of(t * TILE, TILE)
            below = (tile_rows + first) > j
            for h in range(heads):
                block = m_ref[h, pl.ds(first, TILE), :]
                column = jnp.sum(jnp.where(pick, block[:, :n], 0.0), axis=1, keepdims=True)
                column = jnp.where(below, column * scales[h], 0.0)
                m_ref[h, pl.ds(first, TILE), :] = block - column * rows[h]
            return inner

        lax.fori_loop((j + 1) // TILE, n // TILE, update, 0)
        return carry

    lax.fori_loop(0, n, step, 0)
    upper = lax.broadcasted_iota(jnp.int32, (n, n), 0) <= lax.broadcasted_iota(jnp.int32, (n, n), 1)
    for h in range(heads):
        u_ref[h] = jnp.where(upper, m_ref[h, :, :n], 0.0)
        li_ref[h] = m_ref[h, :, n:]


def factor(gram):
    heads, n, _ = gram.shape
    shape = jax.ShapeDtypeStruct((heads, n, n), jnp.float32)
    return pl.pallas_call(
        factor_kernel,
        out_shape=(shape, shape),
        in_specs=[pl.BlockSpec(memory_space=pltpu.VMEM)],
        out_specs=(pl.BlockSpec(memory_space=pltpu.VMEM), pl.BlockSpec(memory_space=pltpu.VMEM)),
        scratch_shapes=[pltpu.VMEM((heads, n, 2 * n), jnp.float32)],
    )(gram)


def fold_pairs(gram):
    heads, n, _ = gram.shape
    upper = lax.broadcasted_iota(jnp.int32, (n, n), 0) <= lax.broadcasted_iota(jnp.int32, (n, n), 1)
    first, second = gram[0::2], gram[1::2]
    square = jnp.where(upper[None], first, second)
    diagonal = jnp.diagonal(second, axis1=1, axis2=2)[:, None, :]
    return jnp.concatenate([square, diagonal], axis=1)


def unfold_pairs(folded):
    pairs, _, n = folded.shape
    square, diagonal = folded[:, :n, :], folded[:, n, :]
    rows = lax.broadcasted_iota(jnp.int32, (n, n), 0)
    cols = lax.broadcasted_iota(jnp.int32, (n, n), 1)
    upper_part = jnp.where((rows <= cols)[None], square, 0.0)
    first = upper_part + jnp.swapaxes(jnp.where((rows < cols)[None], square, 0.0), 1, 2)
    lower_part = jnp.where((rows > cols)[None], square, 0.0)
    second = lower_part + jnp.swapaxes(lower_part, 1, 2) + jnp.where((rows == cols)[None], diagonal[:, None, :], 0.0)
    return jnp.stack([first, second], axis=1).reshape(2 * pairs, n, n)


def exchange_sum(value, axis):
    count = lax.axis_size(axis)
    step = 1
    while step < count:
        partner = lax.ppermute(value, axis, [(i, i ^ step) for i in range(count)])
        value = value + partner
        step *= 2
    return value


def exchange_gather(value, axis):
    count = lax.axis_size(axis)
    me = lax.axis_index(axis)
    step = 1
    while step < count:
        partner = lax.ppermute(value, axis, [(i, i ^ step) for i in range(count)])
        low = (me & step) == 0
        first = jnp.where(low, value, partner)
        second = jnp.where(low, partner, value)
        value = jnp.concatenate([first, second], axis=0)
        step *= 2
    return value


def positions_and_docs(block_pos, doc_offset):
    block_total = block_pos.shape[0]
    doc_flags = (doc_offset < BLOCK).astype(jnp.int32)
    starts_before = jnp.cumsum(doc_flags) - doc_flags
    matches = block_pos[:, None] == jnp.arange(block_total, dtype=jnp.int32)[None, :]
    start_count = jnp.sum(jnp.where(matches, starts_before[None, :], 0), axis=1)
    offsets = jnp.sum(jnp.where(matches, doc_offset[None, :], 0), axis=1)
    within = jnp.arange(BLOCK, dtype=jnp.int32)
    seq_pos = (block_pos[:, None] * BLOCK + within[None, :]).reshape(-1)
    doc_id = (
        start_count[:, None] + (within[None, :] >= offsets[:, None]).astype(jnp.int32)
    ).reshape(-1)
    return (seq_pos, doc_id)


def gram_of(matrix):
    return jnp.einsum("hnc,hnd->hcd", matrix, matrix, precision=lax.Precision.HIGHEST)


SEQ = ("y", "x")
HEAD = ("z", "c")


def local(queries, keys, values, residual, norm_gain, block_pos, doc_offset):
    row_count = queries.shape[0]
    head_count = queries.shape[1] // HD
    group_size = HEADS // KVH
    share_count = max(1, head_count // group_size)
    per_share = head_count // share_count
    total_rows = row_count * lax.axis_size(SEQ)
    global_first = lax.axis_index(HEAD) * head_count
    copy_index = global_first // HEADS
    first_head = global_first % HEADS
    first_share = first_head // group_size
    key_start = copy_index * (KVH * HD) + first_share * HD
    key_cols = lax.dynamic_slice_in_dim(keys, key_start, share_count * HD, 1)
    value_cols = lax.dynamic_slice_in_dim(values, key_start, share_count * HD, 1)
    own_blocks = lax.dynamic_index_in_dim(block_pos, copy_index, 0, keepdims=False)
    own_offsets = lax.dynamic_index_in_dim(doc_offset, copy_index, 0, keepdims=False)
    gain_cols = lax.dynamic_slice_in_dim(norm_gain, first_head * HD, head_count * HD)
    seq_pos, doc_id = positions_and_docs(own_blocks, own_offsets)
    first_row = lax.axis_index(SEQ) * row_count
    own_pos = lax.dynamic_slice_in_dim(seq_pos, first_row, row_count)
    own_doc = lax.dynamic_slice_in_dim(doc_id, first_row, row_count)
    query_heads = queries.reshape(row_count, share_count, per_share, HD)
    score_scale = 1.0 / math.sqrt(HD)

    def attend_block(state_now, key_piece, value_piece, first_key):
        length = key_piece.shape[0]
        key_pos = lax.dynamic_slice_in_dim(seq_pos, first_key, length)
        key_doc = lax.dynamic_slice_in_dim(doc_id, first_key, length)
        seen = (key_pos[None, :] <= own_pos[:, None]) & (key_doc[None, :] == own_doc[:, None])

        def accumulate(state_inner):
            run_max, run_total, run_acc = state_inner
            key_heads = key_piece.reshape(length, share_count, HD)
            value_heads = value_piece.reshape(length, share_count, HD)
            scores = (
                jnp.einsum(
                    "rkgd,nkd->kgrn", query_heads, key_heads, preferred_element_type=jnp.float32
                )
                * score_scale
            )
            scores = jnp.where(seen[None, None], scores, -jnp.inf)
            new_max = jnp.maximum(run_max, jnp.max(scores, axis=3))
            factor = jnp.exp(run_max - new_max)
            expo = jnp.exp(scores - new_max[..., None])
            new_total = run_total * factor + jnp.sum(expo, axis=3)
            partial_value = jnp.einsum(
                "kgrn,nkd->kgrd",
                expo.astype(jnp.bfloat16),
                value_heads,
                preferred_element_type=jnp.float32,
            )
            new_acc = run_acc * factor[..., None] + partial_value
            return (new_max, new_total, new_acc)

        def unchanged(state_inner):
            return state_inner

        return lax.cond(jnp.any(seen), accumulate, unchanged, state_now)

    start_state = (
        jnp.full((share_count, per_share, row_count), -1e30, jnp.float32),
        jnp.zeros((share_count, per_share, row_count), jnp.float32),
        jnp.zeros((share_count, per_share, row_count, HD), jnp.float32),
    )
    core = lax.axis_index("c")
    mine = jnp.where(core == 0, key_cols, value_cols)
    gathered = lax.all_gather(exchange_gather(mine, "x"), "y", axis=0, tiled=True)
    other = lax.ppermute(gathered, "c", perm=[(0, 1), (1, 0)])
    key_piece = jnp.where(core == 0, gathered, other)
    value_piece = jnp.where(core == 0, other, gathered)
    length = key_piece.shape[0]
    step_rows = math.gcd(length, 1024)

    def advance(step_index, state_inner):
        begin_row = step_index * step_rows
        key_part = lax.dynamic_slice_in_dim(key_piece, begin_row, step_rows, 0)
        value_part = lax.dynamic_slice_in_dim(value_piece, begin_row, step_rows, 0)
        return attend_block(state_inner, key_part, value_part, begin_row)

    final_max, final_total, final_acc = lax.fori_loop(0, length // step_rows, advance, start_state)
    output = final_acc / final_total[..., None]
    attn_out = (
        jnp.transpose(output, (2, 0, 1, 3)).reshape(row_count, head_count * HD).astype(jnp.bfloat16)
    )
    mixed = attn_out.astype(jnp.float32) + residual.astype(jnp.float32)
    local_squares = jnp.sum(mixed * mixed, axis=1)
    slot_mask = jnp.arange(COPIES, dtype=jnp.int32) == copy_index
    slotted = jnp.where(slot_mask[:, None], local_squares[None, :], 0.0)
    summed = over_copies(slotted, HEAD)
    square_sum = lax.dynamic_index_in_dim(summed, copy_index, 0, keepdims=False)
    normed = mixed * lax.rsqrt(square_sum[:, None] / WIDTH + EPSILON) * gain_cols[None, :]
    blocks = normed.reshape(row_count, head_count, HD)
    head_rows = jnp.transpose(blocks, (1, 0, 2))
    gram_sum = unfold_pairs(exchange_sum(exchange_sum(fold_pairs(gram_of(head_rows)), "x"), "y"))
    upper_factor, lower_inverse = factor(gram_sum)
    r_factor = upper_factor / math.sqrt(total_rows)
    solved = jnp.einsum("rhc,hdc->rhd", blocks, lower_inverse, precision=lax.Precision.HIGHEST)
    whitened = solved.reshape(row_count, head_count * HD) * math.sqrt(total_rows)
    return (attn_out, r_factor, whitened)


def solution(mesh):
    seq_size, head_size = mesh.devices.shape
    side = math.isqrt(seq_size)
    grid = jax.sharding.Mesh(
        mesh.devices.reshape(side, seq_size // side, head_size // 2, 2), ("y", "x", "z", "c")
    )
    return jax.shard_map(
        local,
        mesh=grid,
        in_specs=(
            P(SEQ, HEAD),
            P(SEQ, None),
            P(SEQ, None),
            P(SEQ, HEAD),
            P(),
            P(),
            P(),
        ),
        out_specs=(P(SEQ, HEAD), P(HEAD, None, None), P(SEQ, HEAD)),
        check_vma=False,
    )
```

```python
import math

import jax
import jax.numpy as jnp
from jax import lax
from jax.experimental import pallas as pl
from jax.experimental.pallas import tpu as pltpu
from jax.sharding import PartitionSpec as P

HEADS = 64
KVH = 8
HD = 128
BLOCK = 128
COPIES = 1
WIDTH = 8192


EPSILON = 1e-05


def side_by_side(arrays, axis, dim, along):
    both = jnp.concatenate(arrays, axis=along)
    whole, at, done = (lax.all_gather(both, axis, axis=dim, tiled=True), 0, [])
    for a in arrays:
        done.append(lax.slice_in_dim(whole, at, at + a.shape[along], axis=along))
        at += a.shape[along]
    return tuple(done)


def copy_for_each(shard, axis):
    count = lax.axis_size(axis)
    return lax.all_to_all(
        jnp.broadcast_to(shard[None], (count, *shard.shape)), axis, 0, 0, tiled=True
    )


def over_copies(shard, axis):
    everything = copy_for_each(shard, axis)
    return jnp.sum(everything, axis=0)


def factor_kernel(g_ref, u_ref, li_ref, m_ref):
    heads, n, _ = g_ref.shape
    row_ids = lax.broadcasted_iota(jnp.int32, (n, 1), 0)
    lane_ids = lax.broadcasted_iota(jnp.int32, (1, n), 1)
    eye = (lax.broadcasted_iota(jnp.int32, (n, n), 0) == lax.broadcasted_iota(jnp.int32, (n, n), 1)).astype(jnp.float32)
    for h in range(heads):
        m_ref[h, :, :n] = g_ref[h]
        m_ref[h, :, n:] = eye
    spare = jnp.zeros((8 - heads, n), jnp.float32)

    def step(j, carry):
        pick = lane_ids == j
        below = row_ids > j
        rows = [m_ref[h, pl.ds(j, 1), :] for h in range(heads)]
        columns = jnp.transpose(jnp.concatenate([r[:, :n] for r in rows] + [spare], axis=0))
        for h in range(heads):
            pivot = jnp.sum(jnp.where(pick, rows[h][:, :n], 0.0), axis=1, keepdims=True)
            scale = lax.rsqrt(pivot)
            scaled = rows[h] * scale
            column = jnp.where(below, columns[:, h : h + 1] * scale, 0.0)
            m_ref[h] = m_ref[h] - column * scaled
            m_ref[h, pl.ds(j, 1), :] = scaled
        return carry

    lax.fori_loop(0, n, step, 0)
    upper = lax.broadcasted_iota(jnp.int32, (n, n), 0) <= lax.broadcasted_iota(jnp.int32, (n, n), 1)
    for h in range(heads):
        u_ref[h] = jnp.where(upper, m_ref[h, :, :n], 0.0)
        li_ref[h] = m_ref[h, :, n:]


def factor(gram):
    heads, n, _ = gram.shape
    shape = jax.ShapeDtypeStruct((heads, n, n), jnp.float32)
    return pl.pallas_call(
        factor_kernel,
        out_shape=(shape, shape),
        in_specs=[pl.BlockSpec(memory_space=pltpu.VMEM)],
        out_specs=(pl.BlockSpec(memory_space=pltpu.VMEM), pl.BlockSpec(memory_space=pltpu.VMEM)),
        scratch_shapes=[pltpu.VMEM((heads, n, 2 * n), jnp.float32)],
    )(gram)


def fold_pairs(gram):
    heads, n, _ = gram.shape
    upper = lax.broadcasted_iota(jnp.int32, (n, n), 0) <= lax.broadcasted_iota(jnp.int32, (n, n), 1)
    first, second = gram[0::2], gram[1::2]
    square = jnp.where(upper[None], first, second)
    diagonal = jnp.diagonal(second, axis1=1, axis2=2)[:, None, :]
    return jnp.concatenate([square, diagonal], axis=1)


def unfold_pairs(folded):
    pairs, _, n = folded.shape
    square, diagonal = folded[:, :n, :], folded[:, n, :]
    rows = lax.broadcasted_iota(jnp.int32, (n, n), 0)
    cols = lax.broadcasted_iota(jnp.int32, (n, n), 1)
    upper_part = jnp.where((rows <= cols)[None], square, 0.0)
    first = upper_part + jnp.swapaxes(jnp.where((rows < cols)[None], square, 0.0), 1, 2)
    lower_part = jnp.where((rows > cols)[None], square, 0.0)
    second = lower_part + jnp.swapaxes(lower_part, 1, 2) + jnp.where((rows == cols)[None], diagonal[:, None, :], 0.0)
    return jnp.stack([first, second], axis=1).reshape(2 * pairs, n, n)


def exchange_sum(value, axis):
    count = lax.axis_size(axis)
    step = 1
    while step < count:
        partner = lax.ppermute(value, axis, [(i, i ^ step) for i in range(count)])
        value = value + partner
        step *= 2
    return value


def exchange_gather(value, axis):
    count = lax.axis_size(axis)
    me = lax.axis_index(axis)
    step = 1
    while step < count:
        partner = lax.ppermute(value, axis, [(i, i ^ step) for i in range(count)])
        low = (me & step) == 0
        first = jnp.where(low, value, partner)
        second = jnp.where(low, partner, value)
        value = jnp.concatenate([first, second], axis=0)
        step *= 2
    return value


def positions_and_docs(block_pos, doc_offset):
    block_total = block_pos.shape[0]
    doc_flags = (doc_offset < BLOCK).astype(jnp.int32)
    starts_before = jnp.cumsum(doc_flags) - doc_flags
    matches = block_pos[:, None] == jnp.arange(block_total, dtype=jnp.int32)[None, :]
    start_count = jnp.sum(jnp.where(matches, starts_before[None, :], 0), axis=1)
    offsets = jnp.sum(jnp.where(matches, doc_offset[None, :], 0), axis=1)
    within = jnp.arange(BLOCK, dtype=jnp.int32)
    seq_pos = (block_pos[:, None] * BLOCK + within[None, :]).reshape(-1)
    doc_id = (
        start_count[:, None] + (within[None, :] >= offsets[:, None]).astype(jnp.int32)
    ).reshape(-1)
    return (seq_pos, doc_id)


def gram_of(matrix):
    return jnp.einsum("hnc,hnd->hcd", matrix, matrix, precision=lax.Precision.HIGHEST)


SEQ = ("y", "x")
HEAD = ("z", "c")


def local(queries, keys, values, residual, norm_gain, block_pos, doc_offset):
    row_count = queries.shape[0]
    head_count = queries.shape[1] // HD
    group_size = HEADS // KVH
    share_count = max(1, head_count // group_size)
    per_share = head_count // share_count
    total_rows = row_count * lax.axis_size(SEQ)
    global_first = lax.axis_index(HEAD) * head_count
    copy_index = global_first // HEADS
    first_head = global_first % HEADS
    first_share = first_head // group_size
    key_start = copy_index * (KVH * HD) + first_share * HD
    key_cols = lax.dynamic_slice_in_dim(keys, key_start, share_count * HD, 1)
    value_cols = lax.dynamic_slice_in_dim(values, key_start, share_count * HD, 1)
    own_blocks = lax.dynamic_index_in_dim(block_pos, copy_index, 0, keepdims=False)
    own_offsets = lax.dynamic_index_in_dim(doc_offset, copy_index, 0, keepdims=False)
    gain_cols = lax.dynamic_slice_in_dim(norm_gain, first_head * HD, head_count * HD)
    seq_pos, doc_id = positions_and_docs(own_blocks, own_offsets)
    first_row = lax.axis_index(SEQ) * row_count
    own_pos = lax.dynamic_slice_in_dim(seq_pos, first_row, row_count)
    own_doc = lax.dynamic_slice_in_dim(doc_id, first_row, row_count)
    query_heads = queries.reshape(row_count, share_count, per_share, HD)
    score_scale = 1.0 / math.sqrt(HD)

    def attend_block(state_now, key_piece, value_piece, first_key):
        length = key_piece.shape[0]
        key_pos = lax.dynamic_slice_in_dim(seq_pos, first_key, length)
        key_doc = lax.dynamic_slice_in_dim(doc_id, first_key, length)
        seen = (key_pos[None, :] <= own_pos[:, None]) & (key_doc[None, :] == own_doc[:, None])

        def accumulate(state_inner):
            run_max, run_total, run_acc = state_inner
            key_heads = key_piece.reshape(length, share_count, HD)
            value_heads = value_piece.reshape(length, share_count, HD)
            scores = (
                jnp.einsum(
                    "rkgd,nkd->kgrn", query_heads, key_heads, preferred_element_type=jnp.float32
                )
                * score_scale
            )
            scores = jnp.where(seen[None, None], scores, -jnp.inf)
            new_max = jnp.maximum(run_max, jnp.max(scores, axis=3))
            factor = jnp.exp(run_max - new_max)
            expo = jnp.exp(scores - new_max[..., None])
            new_total = run_total * factor + jnp.sum(expo, axis=3)
            partial_value = jnp.einsum(
                "kgrn,nkd->kgrd",
                expo.astype(jnp.bfloat16),
                value_heads,
                preferred_element_type=jnp.float32,
            )
            new_acc = run_acc * factor[..., None] + partial_value
            return (new_max, new_total, new_acc)

        def unchanged(state_inner):
            return state_inner

        return lax.cond(jnp.any(seen), accumulate, unchanged, state_now)

    start_state = (
        jnp.full((share_count, per_share, row_count), -1e30, jnp.float32),
        jnp.zeros((share_count, per_share, row_count), jnp.float32),
        jnp.zeros((share_count, per_share, row_count, HD), jnp.float32),
    )
    core = lax.axis_index("c")
    mine = jnp.where(core == 0, key_cols, value_cols)
    gathered = lax.all_gather(exchange_gather(mine, "x"), "y", axis=0, tiled=True)
    other = lax.ppermute(gathered, "c", perm=[(0, 1), (1, 0)])
    key_piece = jnp.where(core == 0, gathered, other)
    value_piece = jnp.where(core == 0, other, gathered)
    length = key_piece.shape[0]
    step_rows = math.gcd(length, 1024)

    def advance(step_index, state_inner):
        begin_row = step_index * step_rows
        key_part = lax.dynamic_slice_in_dim(key_piece, begin_row, step_rows, 0)
        value_part = lax.dynamic_slice_in_dim(value_piece, begin_row, step_rows, 0)
        return attend_block(state_inner, key_part, value_part, begin_row)

    final_max, final_total, final_acc = lax.fori_loop(0, length // step_rows, advance, start_state)
    output = final_acc / final_total[..., None]
    attn_out = (
        jnp.transpose(output, (2, 0, 1, 3)).reshape(row_count, head_count * HD).astype(jnp.bfloat16)
    )
    mixed = attn_out.astype(jnp.float32) + residual.astype(jnp.float32)
    local_squares = jnp.sum(mixed * mixed, axis=1)
    slot_mask = jnp.arange(COPIES, dtype=jnp.int32) == copy_index
    slotted = jnp.where(slot_mask[:, None], local_squares[None, :], 0.0)
    summed = over_copies(slotted, HEAD)
    square_sum = lax.dynamic_index_in_dim(summed, copy_index, 0, keepdims=False)
    normed = mixed * lax.rsqrt(square_sum[:, None] / WIDTH + EPSILON) * gain_cols[None, :]
    blocks = normed.reshape(row_count, head_count, HD)
    head_rows = jnp.transpose(blocks, (1, 0, 2))
    gram_sum = unfold_pairs(exchange_sum(exchange_sum(fold_pairs(gram_of(head_rows)), "x"), "y"))
    upper_factor, lower_inverse = factor(gram_sum)
    r_factor = upper_factor / math.sqrt(total_rows)
    solved = jnp.einsum("rhc,hdc->rhd", blocks, lower_inverse, precision=lax.Precision.HIGHEST)
    whitened = solved.reshape(row_count, head_count * HD) * math.sqrt(total_rows)
    return (attn_out, r_factor, whitened)


def solution(mesh):
    seq_size, head_size = mesh.devices.shape
    side = math.isqrt(seq_size)
    grid = jax.sharding.Mesh(
        mesh.devices.reshape(side, seq_size // side, head_size // 2, 2), ("y", "x", "z", "c")
    )
    return jax.shard_map(
        local,
        mesh=grid,
        in_specs=(
            P(SEQ, HEAD),
            P(SEQ, None),
            P(SEQ, None),
            P(SEQ, HEAD),
            P(),
            P(),
            P(),
        ),
        out_specs=(P(SEQ, HEAD), P(HEAD, None, None), P(SEQ, HEAD)),
        check_vma=False,
    )
```

```python
import math

import jax
import jax.numpy as jnp
from jax import lax
from jax.experimental import pallas as pl
from jax.experimental.pallas import tpu as pltpu
from jax.sharding import PartitionSpec as P

HEADS = 64
KVH = 8
HD = 128
BLOCK = 128
COPIES = 1
WIDTH = 8192


EPSILON = 1e-05


def side_by_side(arrays, axis, dim, along):
    both = jnp.concatenate(arrays, axis=along)
    whole, at, done = (lax.all_gather(both, axis, axis=dim, tiled=True), 0, [])
    for a in arrays:
        done.append(lax.slice_in_dim(whole, at, at + a.shape[along], axis=along))
        at += a.shape[along]
    return tuple(done)


def copy_for_each(shard, axis):
    count = lax.axis_size(axis)
    return lax.all_to_all(
        jnp.broadcast_to(shard[None], (count, *shard.shape)), axis, 0, 0, tiled=True
    )


def over_copies(shard, axis):
    everything = copy_for_each(shard, axis)
    return jnp.sum(everything, axis=0)


PANEL = 16


def factor_kernel(g_ref, u_ref, li_ref, m_ref):
    heads, n, _ = g_ref.shape
    row_ids = lax.broadcasted_iota(jnp.int32, (n, 1), 0)
    lane_ids = lax.broadcasted_iota(jnp.int32, (1, n), 1)
    panel_rows = lax.broadcasted_iota(jnp.int32, (PANEL, 1), 0)
    eye = (lax.broadcasted_iota(jnp.int32, (n, n), 0) == lax.broadcasted_iota(jnp.int32, (n, n), 1)).astype(jnp.float32)
    for h in range(heads):
        m_ref[h, :, :n] = g_ref[h]
        m_ref[h, :, n:] = eye
    spare = jnp.zeros((8 - heads, n), jnp.float32)

    for top in range(0, n, PANEL):

        def step(offset, carry, top=top):
            j = top + offset
            pick = lane_ids == j
            below = (panel_rows + top) > j
            rows = [m_ref[h, pl.ds(j, 1), :] for h in range(heads)]
            columns = jnp.transpose(jnp.concatenate([r[:, :n] for r in rows] + [spare], axis=0))
            columns = columns[top : top + PANEL]
            for h in range(heads):
                pivot = jnp.sum(jnp.where(pick, rows[h][:, :n], 0.0), axis=1, keepdims=True)
                scale = lax.rsqrt(pivot)
                scaled = rows[h] * scale
                column = jnp.where(below, columns[:, h : h + 1] * scale, 0.0)
                block = m_ref[h, top : top + PANEL, :]
                m_ref[h, top : top + PANEL, :] = block - column * scaled
                m_ref[h, pl.ds(j, 1), :] = scaled
            return carry

        lax.fori_loop(0, PANEL, step, 0)
        if top + PANEL < n:
            for h in range(heads):
                panel = m_ref[h, top : top + PANEL, :]
                lead = jnp.where(row_ids >= top + PANEL, jnp.transpose(panel[:, :n]), 0.0)
                m_ref[h] = m_ref[h] - jnp.dot(
                    lead, panel, precision=lax.Precision.HIGHEST, preferred_element_type=jnp.float32
                )
    upper = lax.broadcasted_iota(jnp.int32, (n, n), 0) <= lax.broadcasted_iota(jnp.int32, (n, n), 1)
    for h in range(heads):
        u_ref[h] = jnp.where(upper, m_ref[h, :, :n], 0.0)
        li_ref[h] = m_ref[h, :, n:]


def factor(gram):
    heads, n, _ = gram.shape
    shape = jax.ShapeDtypeStruct((heads, n, n), jnp.float32)
    return pl.pallas_call(
        factor_kernel,
        out_shape=(shape, shape),
        in_specs=[pl.BlockSpec(memory_space=pltpu.VMEM)],
        out_specs=(pl.BlockSpec(memory_space=pltpu.VMEM), pl.BlockSpec(memory_space=pltpu.VMEM)),
        scratch_shapes=[pltpu.VMEM((heads, n, 2 * n), jnp.float32)],
    )(gram)


def fold_pairs(gram):
    heads, n, _ = gram.shape
    upper = lax.broadcasted_iota(jnp.int32, (n, n), 0) <= lax.broadcasted_iota(jnp.int32, (n, n), 1)
    first, second = gram[0::2], gram[1::2]
    square = jnp.where(upper[None], first, second)
    diagonal = jnp.diagonal(second, axis1=1, axis2=2)[:, None, :]
    return jnp.concatenate([square, diagonal], axis=1)


def unfold_pairs(folded):
    pairs, _, n = folded.shape
    square, diagonal = folded[:, :n, :], folded[:, n, :]
    rows = lax.broadcasted_iota(jnp.int32, (n, n), 0)
    cols = lax.broadcasted_iota(jnp.int32, (n, n), 1)
    upper_part = jnp.where((rows <= cols)[None], square, 0.0)
    first = upper_part + jnp.swapaxes(jnp.where((rows < cols)[None], square, 0.0), 1, 2)
    lower_part = jnp.where((rows > cols)[None], square, 0.0)
    second = lower_part + jnp.swapaxes(lower_part, 1, 2) + jnp.where((rows == cols)[None], diagonal[:, None, :], 0.0)
    return jnp.stack([first, second], axis=1).reshape(2 * pairs, n, n)


def exchange_sum(value, axis):
    count = lax.axis_size(axis)
    step = 1
    while step < count:
        partner = lax.ppermute(value, axis, [(i, i ^ step) for i in range(count)])
        value = value + partner
        step *= 2
    return value


def exchange_gather(value, axis):
    count = lax.axis_size(axis)
    me = lax.axis_index(axis)
    step = 1
    while step < count:
        partner = lax.ppermute(value, axis, [(i, i ^ step) for i in range(count)])
        low = (me & step) == 0
        first = jnp.where(low, value, partner)
        second = jnp.where(low, partner, value)
        value = jnp.concatenate([first, second], axis=0)
        step *= 2
    return value


def positions_and_docs(block_pos, doc_offset):
    block_total = block_pos.shape[0]
    doc_flags = (doc_offset < BLOCK).astype(jnp.int32)
    starts_before = jnp.cumsum(doc_flags) - doc_flags
    matches = block_pos[:, None] == jnp.arange(block_total, dtype=jnp.int32)[None, :]
    start_count = jnp.sum(jnp.where(matches, starts_before[None, :], 0), axis=1)
    offsets = jnp.sum(jnp.where(matches, doc_offset[None, :], 0), axis=1)
    within = jnp.arange(BLOCK, dtype=jnp.int32)
    seq_pos = (block_pos[:, None] * BLOCK + within[None, :]).reshape(-1)
    doc_id = (
        start_count[:, None] + (within[None, :] >= offsets[:, None]).astype(jnp.int32)
    ).reshape(-1)
    return (seq_pos, doc_id)


def gram_of(matrix):
    return jnp.einsum("hnc,hnd->hcd", matrix, matrix, precision=lax.Precision.HIGHEST)


SEQ = ("y", "x")
HEAD = ("z", "c")


def local(queries, keys, values, residual, norm_gain, block_pos, doc_offset):
    row_count = queries.shape[0]
    head_count = queries.shape[1] // HD
    group_size = HEADS // KVH
    share_count = max(1, head_count // group_size)
    per_share = head_count // share_count
    total_rows = row_count * lax.axis_size(SEQ)
    global_first = lax.axis_index(HEAD) * head_count
    copy_index = global_first // HEADS
    first_head = global_first % HEADS
    first_share = first_head // group_size
    key_start = copy_index * (KVH * HD) + first_share * HD
    key_cols = lax.dynamic_slice_in_dim(keys, key_start, share_count * HD, 1)
    value_cols = lax.dynamic_slice_in_dim(values, key_start, share_count * HD, 1)
    own_blocks = lax.dynamic_index_in_dim(block_pos, copy_index, 0, keepdims=False)
    own_offsets = lax.dynamic_index_in_dim(doc_offset, copy_index, 0, keepdims=False)
    gain_cols = lax.dynamic_slice_in_dim(norm_gain, first_head * HD, head_count * HD)
    seq_pos, doc_id = positions_and_docs(own_blocks, own_offsets)
    first_row = lax.axis_index(SEQ) * row_count
    own_pos = lax.dynamic_slice_in_dim(seq_pos, first_row, row_count)
    own_doc = lax.dynamic_slice_in_dim(doc_id, first_row, row_count)
    query_heads = queries.reshape(row_count, share_count, per_share, HD)
    score_scale = 1.0 / math.sqrt(HD)

    def attend_block(state_now, key_piece, value_piece, first_key):
        length = key_piece.shape[0]
        key_pos = lax.dynamic_slice_in_dim(seq_pos, first_key, length)
        key_doc = lax.dynamic_slice_in_dim(doc_id, first_key, length)
        seen = (key_pos[None, :] <= own_pos[:, None]) & (key_doc[None, :] == own_doc[:, None])

        def accumulate(state_inner):
            run_max, run_total, run_acc = state_inner
            key_heads = key_piece.reshape(length, share_count, HD)
            value_heads = value_piece.reshape(length, share_count, HD)
            scores = (
                jnp.einsum(
                    "rkgd,nkd->kgrn", query_heads, key_heads, preferred_element_type=jnp.float32
                )
                * score_scale
            )
            scores = jnp.where(seen[None, None], scores, -jnp.inf)
            new_max = jnp.maximum(run_max, jnp.max(scores, axis=3))
            factor = jnp.exp(run_max - new_max)
            expo = jnp.exp(scores - new_max[..., None])
            new_total = run_total * factor + jnp.sum(expo, axis=3)
            partial_value = jnp.einsum(
                "kgrn,nkd->kgrd",
                expo.astype(jnp.bfloat16),
                value_heads,
                preferred_element_type=jnp.float32,
            )
            new_acc = run_acc * factor[..., None] + partial_value
            return (new_max, new_total, new_acc)

        def unchanged(state_inner):
            return state_inner

        return lax.cond(jnp.any(seen), accumulate, unchanged, state_now)

    start_state = (
        jnp.full((share_count, per_share, row_count), -1e30, jnp.float32),
        jnp.zeros((share_count, per_share, row_count), jnp.float32),
        jnp.zeros((share_count, per_share, row_count, HD), jnp.float32),
    )
    core = lax.axis_index("c")
    mine = jnp.where(core == 0, key_cols, value_cols)
    gathered = lax.all_gather(exchange_gather(mine, "x"), "y", axis=0, tiled=True)
    other = lax.ppermute(gathered, "c", perm=[(0, 1), (1, 0)])
    key_piece = jnp.where(core == 0, gathered, other)
    value_piece = jnp.where(core == 0, other, gathered)
    length = key_piece.shape[0]
    step_rows = math.gcd(length, 1024)

    def advance(step_index, state_inner):
        begin_row = step_index * step_rows
        key_part = lax.dynamic_slice_in_dim(key_piece, begin_row, step_rows, 0)
        value_part = lax.dynamic_slice_in_dim(value_piece, begin_row, step_rows, 0)
        return attend_block(state_inner, key_part, value_part, begin_row)

    final_max, final_total, final_acc = lax.fori_loop(0, length // step_rows, advance, start_state)
    output = final_acc / final_total[..., None]
    attn_out = (
        jnp.transpose(output, (2, 0, 1, 3)).reshape(row_count, head_count * HD).astype(jnp.bfloat16)
    )
    mixed = attn_out.astype(jnp.float32) + residual.astype(jnp.float32)
    local_squares = jnp.sum(mixed * mixed, axis=1)
    slot_mask = jnp.arange(COPIES, dtype=jnp.int32) == copy_index
    slotted = jnp.where(slot_mask[:, None], local_squares[None, :], 0.0)
    summed = over_copies(slotted, HEAD)
    square_sum = lax.dynamic_index_in_dim(summed, copy_index, 0, keepdims=False)
    normed = mixed * lax.rsqrt(square_sum[:, None] / WIDTH + EPSILON) * gain_cols[None, :]
    blocks = normed.reshape(row_count, head_count, HD)
    head_rows = jnp.transpose(blocks, (1, 0, 2))
    gram_sum = unfold_pairs(exchange_sum(exchange_sum(fold_pairs(gram_of(head_rows)), "x"), "y"))
    upper_factor, lower_inverse = factor(gram_sum)
    r_factor = upper_factor / math.sqrt(total_rows)
    solved = jnp.einsum("rhc,hdc->rhd", blocks, lower_inverse, precision=lax.Precision.HIGHEST)
    whitened = solved.reshape(row_count, head_count * HD) * math.sqrt(total_rows)
    return (attn_out, r_factor, whitened)


def solution(mesh):
    seq_size, head_size = mesh.devices.shape
    side = math.isqrt(seq_size)
    grid = jax.sharding.Mesh(
        mesh.devices.reshape(side, seq_size // side, head_size // 2, 2), ("y", "x", "z", "c")
    )
    return jax.shard_map(
        local,
        mesh=grid,
        in_specs=(
            P(SEQ, HEAD),
            P(SEQ, None),
            P(SEQ, None),
            P(SEQ, HEAD),
            P(),
            P(),
            P(),
        ),
        out_specs=(P(SEQ, HEAD), P(HEAD, None, None), P(SEQ, HEAD)),
        check_vma=False,
    )
```

```python
import math

import jax
import jax.numpy as jnp
from jax import lax
from jax.experimental import pallas as pl
from jax.experimental.pallas import tpu as pltpu
from jax.sharding import PartitionSpec as P


HEADS = 64
KVH = 8
HD = 128
BLOCK = 128
COPIES = 1
WIDTH = 8192


EPSILON = 1e-05


def side_by_side(arrays, axis, dim, along):
    both = jnp.concatenate(arrays, axis=along)
    whole, at, done = (lax.all_gather(both, axis, axis=dim, tiled=True), 0, [])
    for a in arrays:
        done.append(lax.slice_in_dim(whole, at, at + a.shape[along], axis=along))
        at += a.shape[along]
    return tuple(done)


def copy_for_each(shard, axis):
    count = lax.axis_size(axis)
    return lax.all_to_all(
        jnp.broadcast_to(shard[None], (count, *shard.shape)), axis, 0, 0, tiled=True
    )


def over_copies(shard, axis):
    everything = copy_for_each(shard, axis)
    return jnp.sum(everything, axis=0)


PANEL = 16


def factor_kernel(g_ref, u_ref, li_ref, m_ref):
    heads, n, _ = g_ref.shape
    row_ids = lax.broadcasted_iota(jnp.int32, (n, 1), 0)
    lane_ids = lax.broadcasted_iota(jnp.int32, (1, n), 1)
    panel_rows = lax.broadcasted_iota(jnp.int32, (PANEL, 1), 0)
    eye = (lax.broadcasted_iota(jnp.int32, (n, n), 0) == lax.broadcasted_iota(jnp.int32, (n, n), 1)).astype(jnp.float32)
    for h in range(heads):
        m_ref[h, :, :n] = g_ref[h]
        m_ref[h, :, n:] = eye
    spare = jnp.zeros((8 - heads, n), jnp.float32)

    for top in range(0, n, PANEL):

        def step(offset, carry, top=top):
            j = top + offset
            pick = lane_ids == j
            below = (panel_rows + top) > j
            rows = [m_ref[h, pl.ds(j, 1), :] for h in range(heads)]
            columns = jnp.transpose(jnp.concatenate([r[:, :n] for r in rows] + [spare], axis=0))
            columns = columns[top : top + PANEL]
            for h in range(heads):
                pivot = jnp.sum(jnp.where(pick, rows[h][:, :n], 0.0), axis=1, keepdims=True)
                scale = lax.rsqrt(pivot)
                scaled = rows[h] * scale
                column = jnp.where(below, columns[:, h : h + 1] * scale, 0.0)
                block = m_ref[h, top : top + PANEL, :]
                m_ref[h, top : top + PANEL, :] = block - column * scaled
                m_ref[h, pl.ds(j, 1), :] = scaled
            return carry

        lax.fori_loop(0, PANEL, step, 0)
        if top + PANEL < n:
            for h in range(heads):
                panel = m_ref[h, top : top + PANEL, :]
                lead = jnp.where(row_ids >= top + PANEL, jnp.transpose(panel[:, :n]), 0.0)
                m_ref[h] = m_ref[h] - jnp.dot(
                    lead, panel, precision=lax.Precision.HIGHEST, preferred_element_type=jnp.float32
                )
    upper = lax.broadcasted_iota(jnp.int32, (n, n), 0) <= lax.broadcasted_iota(jnp.int32, (n, n), 1)
    for h in range(heads):
        u_ref[h] = jnp.where(upper, m_ref[h, :, :n], 0.0)
        li_ref[h] = m_ref[h, :, n:]


def factor(gram):
    heads, n, _ = gram.shape
    shape = jax.ShapeDtypeStruct((heads, n, n), jnp.float32)
    return pl.pallas_call(
        factor_kernel,
        out_shape=(shape, shape),
        in_specs=[pl.BlockSpec(memory_space=pltpu.VMEM)],
        out_specs=(pl.BlockSpec(memory_space=pltpu.VMEM), pl.BlockSpec(memory_space=pltpu.VMEM)),
        scratch_shapes=[pltpu.VMEM((heads, n, 2 * n), jnp.float32)],
    )(gram)


def fold_pairs(gram):
    heads, n, _ = gram.shape
    upper = lax.broadcasted_iota(jnp.int32, (n, n), 0) <= lax.broadcasted_iota(jnp.int32, (n, n), 1)
    first, second = gram[0::2], gram[1::2]
    square = jnp.where(upper[None], first, second)
    diagonal = jnp.diagonal(second, axis1=1, axis2=2)[:, None, :]
    return jnp.concatenate([square, diagonal], axis=1)


def unfold_pairs(folded):
    pairs, _, n = folded.shape
    square, diagonal = folded[:, :n, :], folded[:, n, :]
    rows = lax.broadcasted_iota(jnp.int32, (n, n), 0)
    cols = lax.broadcasted_iota(jnp.int32, (n, n), 1)
    upper_part = jnp.where((rows <= cols)[None], square, 0.0)
    first = upper_part + jnp.swapaxes(jnp.where((rows < cols)[None], square, 0.0), 1, 2)
    lower_part = jnp.where((rows > cols)[None], square, 0.0)
    second = lower_part + jnp.swapaxes(lower_part, 1, 2) + jnp.where((rows == cols)[None], diagonal[:, None, :], 0.0)
    return jnp.stack([first, second], axis=1).reshape(2 * pairs, n, n)


def exchange_sum(value, axis):
    count = lax.axis_size(axis)
    level = [value] + [
        lax.ppermute(value, axis, [(i, i ^ step) for i in range(count)]) for step in range(1, count)
    ]
    while len(level) > 1:
        level = [level[k] + level[k + 1] for k in range(0, len(level), 2)]
    return level[0]


def exchange_gather(value, axis):
    count = lax.axis_size(axis)
    me = lax.axis_index(axis)
    level = [value] + [
        lax.ppermute(value, axis, [(i, i ^ step) for i in range(count)]) for step in range(1, count)
    ]
    order = jnp.bitwise_xor(me, jnp.arange(count, dtype=jnp.int32))
    placed = jnp.take(jnp.stack(level), order, axis=0)
    return placed.reshape(count * value.shape[0], *value.shape[1:])


def positions_and_docs(block_pos, doc_offset):
    block_total = block_pos.shape[0]
    doc_flags = (doc_offset < BLOCK).astype(jnp.int32)
    starts_before = jnp.cumsum(doc_flags) - doc_flags
    matches = block_pos[:, None] == jnp.arange(block_total, dtype=jnp.int32)[None, :]
    start_count = jnp.sum(jnp.where(matches, starts_before[None, :], 0), axis=1)
    offsets = jnp.sum(jnp.where(matches, doc_offset[None, :], 0), axis=1)
    within = jnp.arange(BLOCK, dtype=jnp.int32)
    seq_pos = (block_pos[:, None] * BLOCK + within[None, :]).reshape(-1)
    doc_id = (
        start_count[:, None] + (within[None, :] >= offsets[:, None]).astype(jnp.int32)
    ).reshape(-1)
    return (seq_pos, doc_id)


def gram_of(matrix):
    return jnp.einsum("hnc,hnd->hcd", matrix, matrix, precision=lax.Precision.HIGHEST)


SEQ = ("y", "x")
HEAD = ("z", "c")


def local(queries, keys, values, residual, norm_gain, block_pos, doc_offset):
    row_count = queries.shape[0]
    head_count = queries.shape[1] // HD
    group_size = HEADS // KVH
    share_count = max(1, head_count // group_size)
    per_share = head_count // share_count
    total_rows = row_count * lax.axis_size(SEQ)
    global_first = lax.axis_index(HEAD) * head_count
    copy_index = global_first // HEADS
    first_head = global_first % HEADS
    first_share = first_head // group_size
    key_start = copy_index * (KVH * HD) + first_share * HD
    key_cols = lax.dynamic_slice_in_dim(keys, key_start, share_count * HD, 1)
    value_cols = lax.dynamic_slice_in_dim(values, key_start, share_count * HD, 1)
    own_blocks = lax.dynamic_index_in_dim(block_pos, copy_index, 0, keepdims=False)
    own_offsets = lax.dynamic_index_in_dim(doc_offset, copy_index, 0, keepdims=False)
    gain_cols = lax.dynamic_slice_in_dim(norm_gain, first_head * HD, head_count * HD)
    seq_pos, doc_id = positions_and_docs(own_blocks, own_offsets)
    first_row = lax.axis_index(SEQ) * row_count
    own_pos = lax.dynamic_slice_in_dim(seq_pos, first_row, row_count)
    own_doc = lax.dynamic_slice_in_dim(doc_id, first_row, row_count)
    query_heads = queries.reshape(row_count, share_count, per_share, HD)
    score_scale = 1.0 / math.sqrt(HD)

    def attend_block(state_now, key_piece, value_piece, first_key):
        length = key_piece.shape[0]
        key_pos = lax.dynamic_slice_in_dim(seq_pos, first_key, length)
        key_doc = lax.dynamic_slice_in_dim(doc_id, first_key, length)
        seen = (key_pos[None, :] <= own_pos[:, None]) & (key_doc[None, :] == own_doc[:, None])

        def accumulate(state_inner):
            run_max, run_total, run_acc = state_inner
            key_heads = key_piece.reshape(length, share_count, HD)
            value_heads = value_piece.reshape(length, share_count, HD)
            scores = (
                jnp.einsum(
                    "rkgd,nkd->kgrn", query_heads, key_heads, preferred_element_type=jnp.float32
                )
                * score_scale
            )
            scores = jnp.where(seen[None, None], scores, -jnp.inf)
            new_max = jnp.maximum(run_max, jnp.max(scores, axis=3))
            factor = jnp.exp(run_max - new_max)
            expo = jnp.exp(scores - new_max[..., None])
            new_total = run_total * factor + jnp.sum(expo, axis=3)
            partial_value = jnp.einsum(
                "kgrn,nkd->kgrd",
                expo.astype(jnp.bfloat16),
                value_heads,
                preferred_element_type=jnp.float32,
            )
            new_acc = run_acc * factor[..., None] + partial_value
            return (new_max, new_total, new_acc)

        def unchanged(state_inner):
            return state_inner

        return lax.cond(jnp.any(seen), accumulate, unchanged, state_now)

    start_state = (
        jnp.full((share_count, per_share, row_count), -1e30, jnp.float32),
        jnp.zeros((share_count, per_share, row_count), jnp.float32),
        jnp.zeros((share_count, per_share, row_count, HD), jnp.float32),
    )
    core = lax.axis_index("c")
    mine = jnp.where(core == 0, key_cols, value_cols)
    gathered = lax.all_gather(exchange_gather(mine, "x"), "y", axis=0, tiled=True)
    other = lax.ppermute(gathered, "c", perm=[(0, 1), (1, 0)])
    key_piece = jnp.where(core == 0, gathered, other)
    value_piece = jnp.where(core == 0, other, gathered)
    length = key_piece.shape[0]
    step_rows = math.gcd(length, 1024)

    def advance(step_index, state_inner):
        begin_row = step_index * step_rows
        key_part = lax.dynamic_slice_in_dim(key_piece, begin_row, step_rows, 0)
        value_part = lax.dynamic_slice_in_dim(value_piece, begin_row, step_rows, 0)
        return attend_block(state_inner, key_part, value_part, begin_row)

    final_max, final_total, final_acc = lax.fori_loop(0, length // step_rows, advance, start_state)
    output = final_acc / final_total[..., None]
    attn_out = (
        jnp.transpose(output, (2, 0, 1, 3)).reshape(row_count, head_count * HD).astype(jnp.bfloat16)
    )
    mixed = attn_out.astype(jnp.float32) + residual.astype(jnp.float32)
    local_squares = jnp.sum(mixed * mixed, axis=1)
    slot_mask = jnp.arange(COPIES, dtype=jnp.int32) == copy_index
    slotted = jnp.where(slot_mask[:, None], local_squares[None, :], 0.0)
    summed = over_copies(slotted, HEAD)
    square_sum = lax.dynamic_index_in_dim(summed, copy_index, 0, keepdims=False)
    normed = mixed * lax.rsqrt(square_sum[:, None] / WIDTH + EPSILON) * gain_cols[None, :]
    blocks = normed.reshape(row_count, head_count, HD)
    head_rows = jnp.transpose(blocks, (1, 0, 2))
    gram_sum = unfold_pairs(exchange_sum(exchange_sum(fold_pairs(gram_of(head_rows)), "x"), "y"))
    upper_factor, lower_inverse = factor(gram_sum)
    r_factor = upper_factor / math.sqrt(total_rows)
    solved = jnp.einsum("rhc,hdc->rhd", blocks, lower_inverse, precision=lax.Precision.HIGHEST)
    whitened = solved.reshape(row_count, head_count * HD) * math.sqrt(total_rows)
    return (attn_out, r_factor, whitened)


def solution(mesh):
    seq_size, head_size = mesh.devices.shape
    side = math.isqrt(seq_size)
    grid = jax.sharding.Mesh(
        mesh.devices.reshape(side, seq_size // side, head_size // 2, 2), ("y", "x", "z", "c")
    )
    return jax.shard_map(
        local,
        mesh=grid,
        in_specs=(
            P(SEQ, HEAD),
            P(SEQ, None),
            P(SEQ, None),
            P(SEQ, HEAD),
            P(),
            P(),
            P(),
        ),
        out_specs=(P(SEQ, HEAD), P(HEAD, None, None), P(SEQ, HEAD)),
        check_vma=False,
    )
```

```python
import math

import jax
import jax.numpy as jnp
from jax import lax
from jax.experimental import pallas as pl
from jax.experimental.pallas import tpu as pltpu
from jax.sharding import PartitionSpec as P

HEADS = 64
KVH = 8
HD = 128
BLOCK = 128
COPIES = 1
WIDTH = 8192


EPSILON = 1e-05


def side_by_side(arrays, axis, dim, along):
    both = jnp.concatenate(arrays, axis=along)
    whole, at, done = (lax.all_gather(both, axis, axis=dim, tiled=True), 0, [])
    for a in arrays:
        done.append(lax.slice_in_dim(whole, at, at + a.shape[along], axis=along))
        at += a.shape[along]
    return tuple(done)


def copy_for_each(shard, axis):
    count = lax.axis_size(axis)
    return lax.all_to_all(
        jnp.broadcast_to(shard[None], (count, *shard.shape)), axis, 0, 0, tiled=True
    )


def over_copies(shard, axis):
    everything = copy_for_each(shard, axis)
    return jnp.sum(everything, axis=0)


PANEL = 16


def factor_kernel(g_ref, u_ref, li_ref, m_ref):
    heads, n, _ = g_ref.shape
    row_ids = lax.broadcasted_iota(jnp.int32, (n, 1), 0)
    lane_ids = lax.broadcasted_iota(jnp.int32, (1, n), 1)
    panel_rows = lax.broadcasted_iota(jnp.int32, (PANEL, 1), 0)
    eye = (lax.broadcasted_iota(jnp.int32, (n, n), 0) == lax.broadcasted_iota(jnp.int32, (n, n), 1)).astype(jnp.float32)
    for h in range(heads):
        m_ref[h, :, :n] = g_ref[h]
        m_ref[h, :, n:] = eye
    spare = jnp.zeros((8 - heads, n), jnp.float32)

    for top in range(0, n, PANEL):

        def step(offset, carry, top=top):
            j = top + offset
            pick = lane_ids == j
            below = (panel_rows + top) > j
            rows = [m_ref[h, pl.ds(j, 1), :] for h in range(heads)]
            columns = jnp.transpose(jnp.concatenate([r[:, :n] for r in rows] + [spare], axis=0))
            columns = columns[top : top + PANEL]
            for h in range(heads):
                pivot = jnp.sum(jnp.where(pick, rows[h][:, :n], 0.0), axis=1, keepdims=True)
                scale = lax.rsqrt(pivot)
                scaled = rows[h] * scale
                column = jnp.where(below, columns[:, h : h + 1] * scale, 0.0)
                block = m_ref[h, top : top + PANEL, :]
                m_ref[h, top : top + PANEL, :] = block - column * scaled
                m_ref[h, pl.ds(j, 1), :] = scaled
            return carry

        lax.fori_loop(0, PANEL, step, 0)
        if top + PANEL < n:
            for h in range(heads):
                panel = m_ref[h, top : top + PANEL, :]
                lead = jnp.where(row_ids >= top + PANEL, jnp.transpose(panel[:, :n]), 0.0)
                m_ref[h] = m_ref[h] - jnp.dot(
                    lead, panel, precision=lax.Precision.HIGHEST, preferred_element_type=jnp.float32
                )
    upper = lax.broadcasted_iota(jnp.int32, (n, n), 0) <= lax.broadcasted_iota(jnp.int32, (n, n), 1)
    for h in range(heads):
        u_ref[h] = jnp.where(upper, m_ref[h, :, :n], 0.0)
        li_ref[h] = m_ref[h, :, n:]


def factor(gram):
    heads, n, _ = gram.shape
    shape = jax.ShapeDtypeStruct((heads, n, n), jnp.float32)
    return pl.pallas_call(
        factor_kernel,
        out_shape=(shape, shape),
        in_specs=[pl.BlockSpec(memory_space=pltpu.VMEM)],
        out_specs=(pl.BlockSpec(memory_space=pltpu.VMEM), pl.BlockSpec(memory_space=pltpu.VMEM)),
        scratch_shapes=[pltpu.VMEM((heads, n, 2 * n), jnp.float32)],
    )(gram)


def fold_pairs(gram):
    heads, n, _ = gram.shape
    upper = lax.broadcasted_iota(jnp.int32, (n, n), 0) <= lax.broadcasted_iota(jnp.int32, (n, n), 1)
    first, second = gram[0::2], gram[1::2]
    square = jnp.where(upper[None], first, second)
    eye = lax.broadcasted_iota(jnp.int32, (n, n), 0) == lax.broadcasted_iota(jnp.int32, (n, n), 1)
    diagonal = jnp.sum(jnp.where(eye[None], second, 0.0), axis=1, keepdims=True)
    return jnp.concatenate([square, diagonal], axis=1)


def unfold_pairs(folded):
    pairs, _, n = folded.shape
    square, diagonal = folded[:, :n, :], folded[:, n, :]
    rows = lax.broadcasted_iota(jnp.int32, (n, n), 0)
    cols = lax.broadcasted_iota(jnp.int32, (n, n), 1)
    upper_part = jnp.where((rows <= cols)[None], square, 0.0)
    first = upper_part + jnp.swapaxes(jnp.where((rows < cols)[None], square, 0.0), 1, 2)
    lower_part = jnp.where((rows > cols)[None], square, 0.0)
    second = lower_part + jnp.swapaxes(lower_part, 1, 2) + jnp.where((rows == cols)[None], diagonal[:, None, :], 0.0)
    return jnp.stack([first, second], axis=1).reshape(2 * pairs, n, n)


def exchange_sum(value, axis):
    count = lax.axis_size(axis)
    step = 1
    while step < count:
        partner = lax.ppermute(value, axis, [(i, i ^ step) for i in range(count)])
        value = value + partner
        step *= 2
    return value


def exchange_gather(value, axis):
    count = lax.axis_size(axis)
    me = lax.axis_index(axis)
    step = 1
    while step < count:
        partner = lax.ppermute(value, axis, [(i, i ^ step) for i in range(count)])
        low = (me & step) == 0
        first = jnp.where(low, value, partner)
        second = jnp.where(low, partner, value)
        value = jnp.concatenate([first, second], axis=0)
        step *= 2
    return value


def positions_and_docs(block_pos, doc_offset):
    block_total = block_pos.shape[0]
    doc_flags = (doc_offset < BLOCK).astype(jnp.int32)
    starts_before = jnp.cumsum(doc_flags) - doc_flags
    matches = block_pos[:, None] == jnp.arange(block_total, dtype=jnp.int32)[None, :]
    start_count = jnp.sum(jnp.where(matches, starts_before[None, :], 0), axis=1)
    offsets = jnp.sum(jnp.where(matches, doc_offset[None, :], 0), axis=1)
    within = jnp.arange(BLOCK, dtype=jnp.int32)
    seq_pos = (block_pos[:, None] * BLOCK + within[None, :]).reshape(-1)
    doc_id = (
        start_count[:, None] + (within[None, :] >= offsets[:, None]).astype(jnp.int32)
    ).reshape(-1)
    return (seq_pos, doc_id)


def gram_of(matrix):
    return jnp.einsum("hnc,hnd->hcd", matrix, matrix, precision=lax.Precision.HIGHEST)


SEQ = ("y", "x")
HEAD = ("z", "c")


def local(queries, keys, values, residual, norm_gain, block_pos, doc_offset):
    row_count = queries.shape[0]
    head_count = queries.shape[1] // HD
    group_size = HEADS // KVH
    share_count = max(1, head_count // group_size)
    per_share = head_count // share_count
    total_rows = row_count * lax.axis_size(SEQ)
    global_first = lax.axis_index(HEAD) * head_count
    copy_index = global_first // HEADS
    first_head = global_first % HEADS
    first_share = first_head // group_size
    key_start = copy_index * (KVH * HD) + first_share * HD
    key_cols = lax.dynamic_slice_in_dim(keys, key_start, share_count * HD, 1)
    value_cols = lax.dynamic_slice_in_dim(values, key_start, share_count * HD, 1)
    own_blocks = lax.dynamic_index_in_dim(block_pos, copy_index, 0, keepdims=False)
    own_offsets = lax.dynamic_index_in_dim(doc_offset, copy_index, 0, keepdims=False)
    gain_cols = lax.dynamic_slice_in_dim(norm_gain, first_head * HD, head_count * HD)
    seq_pos, doc_id = positions_and_docs(own_blocks, own_offsets)
    first_row = lax.axis_index(SEQ) * row_count
    own_pos = lax.dynamic_slice_in_dim(seq_pos, first_row, row_count)
    own_doc = lax.dynamic_slice_in_dim(doc_id, first_row, row_count)
    query_heads = queries.reshape(row_count, share_count, per_share, HD)
    score_scale = 1.0 / math.sqrt(HD)

    def attend_block(state_now, key_piece, value_piece, first_key):
        length = key_piece.shape[0]
        key_pos = lax.dynamic_slice_in_dim(seq_pos, first_key, length)
        key_doc = lax.dynamic_slice_in_dim(doc_id, first_key, length)
        seen = (key_pos[None, :] <= own_pos[:, None]) & (key_doc[None, :] == own_doc[:, None])

        def accumulate(state_inner):
            run_max, run_total, run_acc = state_inner
            key_heads = key_piece.reshape(length, share_count, HD)
            value_heads = value_piece.reshape(length, share_count, HD)
            scores = (
                jnp.einsum(
                    "rkgd,nkd->kgrn", query_heads, key_heads, preferred_element_type=jnp.float32
                )
                * score_scale
            )
            scores = jnp.where(seen[None, None], scores, -jnp.inf)
            new_max = jnp.maximum(run_max, jnp.max(scores, axis=3))
            factor = jnp.exp(run_max - new_max)
            expo = jnp.exp(scores - new_max[..., None])
            new_total = run_total * factor + jnp.sum(expo, axis=3)
            partial_value = jnp.einsum(
                "kgrn,nkd->kgrd",
                expo.astype(jnp.bfloat16),
                value_heads,
                preferred_element_type=jnp.float32,
            )
            new_acc = run_acc * factor[..., None] + partial_value
            return (new_max, new_total, new_acc)

        def unchanged(state_inner):
            return state_inner

        return lax.cond(jnp.any(seen), accumulate, unchanged, state_now)

    start_state = (
        jnp.full((share_count, per_share, row_count), -1e30, jnp.float32),
        jnp.zeros((share_count, per_share, row_count), jnp.float32),
        jnp.zeros((share_count, per_share, row_count, HD), jnp.float32),
    )
    core = lax.axis_index("c")
    mine = jnp.where(core == 0, key_cols, value_cols)
    gathered = lax.all_gather(exchange_gather(mine, "x"), "y", axis=0, tiled=True)
    other = lax.ppermute(gathered, "c", perm=[(0, 1), (1, 0)])
    key_piece = jnp.where(core == 0, gathered, other)
    value_piece = jnp.where(core == 0, other, gathered)
    length = key_piece.shape[0]
    step_rows = math.gcd(length, 1024)

    def advance(step_index, state_inner):
        begin_row = step_index * step_rows
        key_part = lax.dynamic_slice_in_dim(key_piece, begin_row, step_rows, 0)
        value_part = lax.dynamic_slice_in_dim(value_piece, begin_row, step_rows, 0)
        return attend_block(state_inner, key_part, value_part, begin_row)

    final_max, final_total, final_acc = lax.fori_loop(0, length // step_rows, advance, start_state)
    output = final_acc / final_total[..., None]
    attn_out = (
        jnp.transpose(output, (2, 0, 1, 3)).reshape(row_count, head_count * HD).astype(jnp.bfloat16)
    )
    mixed = attn_out.astype(jnp.float32) + residual.astype(jnp.float32)
    local_squares = jnp.sum(mixed * mixed, axis=1)
    slot_mask = jnp.arange(COPIES, dtype=jnp.int32) == copy_index
    slotted = jnp.where(slot_mask[:, None], local_squares[None, :], 0.0)
    summed = over_copies(slotted, HEAD)
    square_sum = lax.dynamic_index_in_dim(summed, copy_index, 0, keepdims=False)
    normed = mixed * lax.rsqrt(square_sum[:, None] / WIDTH + EPSILON) * gain_cols[None, :]
    blocks = normed.reshape(row_count, head_count, HD)
    head_rows = jnp.transpose(blocks, (1, 0, 2))
    gram_sum = unfold_pairs(exchange_sum(exchange_sum(fold_pairs(gram_of(head_rows)), "x"), "y"))
    upper_factor, lower_inverse = factor(gram_sum)
    r_factor = upper_factor / math.sqrt(total_rows)
    solved = jnp.einsum("rhc,hdc->rhd", blocks, lower_inverse, precision=lax.Precision.HIGHEST)
    whitened = solved.reshape(row_count, head_count * HD) * math.sqrt(total_rows)
    return (attn_out, r_factor, whitened)


def solution(mesh):
    seq_size, head_size = mesh.devices.shape
    side = math.isqrt(seq_size)
    grid = jax.sharding.Mesh(
        mesh.devices.reshape(side, seq_size // side, head_size // 2, 2), ("y", "x", "z", "c")
    )
    return jax.shard_map(
        local,
        mesh=grid,
        in_specs=(
            P(SEQ, HEAD),
            P(SEQ, None),
            P(SEQ, None),
            P(SEQ, HEAD),
            P(),
            P(),
            P(),
        ),
        out_specs=(P(SEQ, HEAD), P(HEAD, None, None), P(SEQ, HEAD)),
        check_vma=False,
    )
```

```python
import math

import jax
import jax.numpy as jnp
from jax import lax
from jax.experimental import pallas as pl
from jax.experimental.pallas import tpu as pltpu
from jax.sharding import PartitionSpec as P

HEADS = 64
KVH = 8
HD = 128
BLOCK = 128
COPIES = 1
WIDTH = 8192


EPSILON = 1e-05


def side_by_side(arrays, axis, dim, along):
    both = jnp.concatenate(arrays, axis=along)
    whole, at, done = (lax.all_gather(both, axis, axis=dim, tiled=True), 0, [])
    for a in arrays:
        done.append(lax.slice_in_dim(whole, at, at + a.shape[along], axis=along))
        at += a.shape[along]
    return tuple(done)


def copy_for_each(shard, axis):
    count = lax.axis_size(axis)
    return lax.all_to_all(
        jnp.broadcast_to(shard[None], (count, *shard.shape)), axis, 0, 0, tiled=True
    )


def over_copies(shard, axis):
    everything = copy_for_each(shard, axis)
    return jnp.sum(everything, axis=0)


PANEL = 32


def factor_kernel(g_ref, u_ref, li_ref, m_ref):
    heads, n, _ = g_ref.shape
    row_ids = lax.broadcasted_iota(jnp.int32, (n, 1), 0)
    lane_ids = lax.broadcasted_iota(jnp.int32, (1, n), 1)
    panel_rows = lax.broadcasted_iota(jnp.int32, (PANEL, 1), 0)
    eye = (lax.broadcasted_iota(jnp.int32, (n, n), 0) == lax.broadcasted_iota(jnp.int32, (n, n), 1)).astype(jnp.float32)
    for h in range(heads):
        m_ref[h, :, :n] = g_ref[h]
        m_ref[h, :, n:] = eye
    spare = jnp.zeros((8 - heads, n), jnp.float32)

    for top in range(0, n, PANEL):

        def step(offset, carry, top=top):
            j = top + offset
            pick = lane_ids == j
            below = (panel_rows + top) > j
            rows = [m_ref[h, pl.ds(j, 1), :] for h in range(heads)]
            columns = jnp.transpose(jnp.concatenate([r[:, :n] for r in rows] + [spare], axis=0))
            columns = columns[top : top + PANEL]
            for h in range(heads):
                pivot = jnp.sum(jnp.where(pick, rows[h][:, :n], 0.0), axis=1, keepdims=True)
                scale = lax.rsqrt(pivot)
                scaled = rows[h] * scale
                column = jnp.where(below, columns[:, h : h + 1] * scale, 0.0)
                block = m_ref[h, top : top + PANEL, :]
                m_ref[h, top : top + PANEL, :] = block - column * scaled
                m_ref[h, pl.ds(j, 1), :] = scaled
            return carry

        lax.fori_loop(0, PANEL, step, 0)
        if top + PANEL < n:
            for h in range(heads):
                panel = m_ref[h, top : top + PANEL, :]
                lead = jnp.where(row_ids >= top + PANEL, jnp.transpose(panel[:, :n]), 0.0)
                m_ref[h] = m_ref[h] - jnp.dot(
                    lead, panel, precision=lax.Precision.HIGHEST, preferred_element_type=jnp.float32
                )
    upper = lax.broadcasted_iota(jnp.int32, (n, n), 0) <= lax.broadcasted_iota(jnp.int32, (n, n), 1)
    for h in range(heads):
        u_ref[h] = jnp.where(upper, m_ref[h, :, :n], 0.0)
        li_ref[h] = m_ref[h, :, n:]


def factor(gram):
    heads, n, _ = gram.shape
    shape = jax.ShapeDtypeStruct((heads, n, n), jnp.float32)
    return pl.pallas_call(
        factor_kernel,
        out_shape=(shape, shape),
        in_specs=[pl.BlockSpec(memory_space=pltpu.VMEM)],
        out_specs=(pl.BlockSpec(memory_space=pltpu.VMEM), pl.BlockSpec(memory_space=pltpu.VMEM)),
        scratch_shapes=[pltpu.VMEM((heads, n, 2 * n), jnp.float32)],
    )(gram)


def fold_pairs(gram):
    heads, n, _ = gram.shape
    upper = lax.broadcasted_iota(jnp.int32, (n, n), 0) <= lax.broadcasted_iota(jnp.int32, (n, n), 1)
    first, second = gram[0::2], gram[1::2]
    square = jnp.where(upper[None], first, second)
    diagonal = jnp.diagonal(second, axis1=1, axis2=2)[:, None, :]
    return jnp.concatenate([square, diagonal], axis=1)


def unfold_pairs(folded):
    pairs, _, n = folded.shape
    square, diagonal = folded[:, :n, :], folded[:, n, :]
    rows = lax.broadcasted_iota(jnp.int32, (n, n), 0)
    cols = lax.broadcasted_iota(jnp.int32, (n, n), 1)
    upper_part = jnp.where((rows <= cols)[None], square, 0.0)
    first = upper_part + jnp.swapaxes(jnp.where((rows < cols)[None], square, 0.0), 1, 2)
    lower_part = jnp.where((rows > cols)[None], square, 0.0)
    second = lower_part + jnp.swapaxes(lower_part, 1, 2) + jnp.where((rows == cols)[None], diagonal[:, None, :], 0.0)
    return jnp.stack([first, second], axis=1).reshape(2 * pairs, n, n)


def exchange_sum(value, axis):
    count = lax.axis_size(axis)
    step = 1
    while step < count:
        partner = lax.ppermute(value, axis, [(i, i ^ step) for i in range(count)])
        value = value + partner
        step *= 2
    return value


def exchange_gather(value, axis):
    count = lax.axis_size(axis)
    me = lax.axis_index(axis)
    step = 1
    while step < count:
        partner = lax.ppermute(value, axis, [(i, i ^ step) for i in range(count)])
        low = (me & step) == 0
        first = jnp.where(low, value, partner)
        second = jnp.where(low, partner, value)
        value = jnp.concatenate([first, second], axis=0)
        step *= 2
    return value


def positions_and_docs(block_pos, doc_offset):
    block_total = block_pos.shape[0]
    doc_flags = (doc_offset < BLOCK).astype(jnp.int32)
    starts_before = jnp.cumsum(doc_flags) - doc_flags
    matches = block_pos[:, None] == jnp.arange(block_total, dtype=jnp.int32)[None, :]
    start_count = jnp.sum(jnp.where(matches, starts_before[None, :], 0), axis=1)
    offsets = jnp.sum(jnp.where(matches, doc_offset[None, :], 0), axis=1)
    within = jnp.arange(BLOCK, dtype=jnp.int32)
    seq_pos = (block_pos[:, None] * BLOCK + within[None, :]).reshape(-1)
    doc_id = (
        start_count[:, None] + (within[None, :] >= offsets[:, None]).astype(jnp.int32)
    ).reshape(-1)
    return (seq_pos, doc_id)


def gram_of(matrix):
    return jnp.einsum("hnc,hnd->hcd", matrix, matrix, precision=lax.Precision.HIGHEST)


SEQ = ("y", "x")
HEAD = ("z", "c")


def local(queries, keys, values, residual, norm_gain, block_pos, doc_offset):
    row_count = queries.shape[0]
    head_count = queries.shape[1] // HD
    group_size = HEADS // KVH
    share_count = max(1, head_count // group_size)
    per_share = head_count // share_count
    total_rows = row_count * lax.axis_size(SEQ)
    global_first = lax.axis_index(HEAD) * head_count
    copy_index = global_first // HEADS
    first_head = global_first % HEADS
    first_share = first_head // group_size
    key_start = copy_index * (KVH * HD) + first_share * HD
    key_cols = lax.dynamic_slice_in_dim(keys, key_start, share_count * HD, 1)
    value_cols = lax.dynamic_slice_in_dim(values, key_start, share_count * HD, 1)
    own_blocks = lax.dynamic_index_in_dim(block_pos, copy_index, 0, keepdims=False)
    own_offsets = lax.dynamic_index_in_dim(doc_offset, copy_index, 0, keepdims=False)
    gain_cols = lax.dynamic_slice_in_dim(norm_gain, first_head * HD, head_count * HD)
    seq_pos, doc_id = positions_and_docs(own_blocks, own_offsets)
    first_row = lax.axis_index(SEQ) * row_count
    own_pos = lax.dynamic_slice_in_dim(seq_pos, first_row, row_count)
    own_doc = lax.dynamic_slice_in_dim(doc_id, first_row, row_count)
    query_heads = queries.reshape(row_count, share_count, per_share, HD)
    score_scale = 1.0 / math.sqrt(HD)

    def attend_block(state_now, key_piece, value_piece, first_key):
        length = key_piece.shape[0]
        key_pos = lax.dynamic_slice_in_dim(seq_pos, first_key, length)
        key_doc = lax.dynamic_slice_in_dim(doc_id, first_key, length)
        seen = (key_pos[None, :] <= own_pos[:, None]) & (key_doc[None, :] == own_doc[:, None])

        def accumulate(state_inner):
            run_max, run_total, run_acc = state_inner
            key_heads = key_piece.reshape(length, share_count, HD)
            value_heads = value_piece.reshape(length, share_count, HD)
            scores = (
                jnp.einsum(
                    "rkgd,nkd->kgrn", query_heads, key_heads, preferred_element_type=jnp.float32
                )
                * score_scale
            )
            scores = jnp.where(seen[None, None], scores, -jnp.inf)
            new_max = jnp.maximum(run_max, jnp.max(scores, axis=3))
            factor = jnp.exp(run_max - new_max)
            expo = jnp.exp(scores - new_max[..., None])
            new_total = run_total * factor + jnp.sum(expo, axis=3)
            partial_value = jnp.einsum(
                "kgrn,nkd->kgrd",
                expo.astype(jnp.bfloat16),
                value_heads,
                preferred_element_type=jnp.float32,
            )
            new_acc = run_acc * factor[..., None] + partial_value
            return (new_max, new_total, new_acc)

        def unchanged(state_inner):
            return state_inner

        return lax.cond(jnp.any(seen), accumulate, unchanged, state_now)

    start_state = (
        jnp.full((share_count, per_share, row_count), -1e30, jnp.float32),
        jnp.zeros((share_count, per_share, row_count), jnp.float32),
        jnp.zeros((share_count, per_share, row_count, HD), jnp.float32),
    )
    core = lax.axis_index("c")
    mine = jnp.where(core == 0, key_cols, value_cols)
    gathered = lax.all_gather(exchange_gather(mine, "x"), "y", axis=0, tiled=True)
    other = lax.ppermute(gathered, "c", perm=[(0, 1), (1, 0)])
    key_piece = jnp.where(core == 0, gathered, other)
    value_piece = jnp.where(core == 0, other, gathered)
    length = key_piece.shape[0]
    step_rows = math.gcd(length, 1024)

    def advance(step_index, state_inner):
        begin_row = step_index * step_rows
        key_part = lax.dynamic_slice_in_dim(key_piece, begin_row, step_rows, 0)
        value_part = lax.dynamic_slice_in_dim(value_piece, begin_row, step_rows, 0)
        return attend_block(state_inner, key_part, value_part, begin_row)

    final_max, final_total, final_acc = lax.fori_loop(0, length // step_rows, advance, start_state)
    output = final_acc / final_total[..., None]
    attn_out = (
        jnp.transpose(output, (2, 0, 1, 3)).reshape(row_count, head_count * HD).astype(jnp.bfloat16)
    )
    mixed = attn_out.astype(jnp.float32) + residual.astype(jnp.float32)
    local_squares = jnp.sum(mixed * mixed, axis=1)
    slot_mask = jnp.arange(COPIES, dtype=jnp.int32) == copy_index
    slotted = jnp.where(slot_mask[:, None], local_squares[None, :], 0.0)
    summed = over_copies(slotted, HEAD)
    square_sum = lax.dynamic_index_in_dim(summed, copy_index, 0, keepdims=False)
    normed = mixed * lax.rsqrt(square_sum[:, None] / WIDTH + EPSILON) * gain_cols[None, :]
    blocks = normed.reshape(row_count, head_count, HD)
    head_rows = jnp.transpose(blocks, (1, 0, 2))
    gram_sum = unfold_pairs(exchange_sum(exchange_sum(fold_pairs(gram_of(head_rows)), "x"), "y"))
    upper_factor, lower_inverse = factor(gram_sum)
    r_factor = upper_factor / math.sqrt(total_rows)
    solved = jnp.einsum("rhc,hdc->rhd", blocks, lower_inverse, precision=lax.Precision.HIGHEST)
    whitened = solved.reshape(row_count, head_count * HD) * math.sqrt(total_rows)
    return (attn_out, r_factor, whitened)


def solution(mesh):
    seq_size, head_size = mesh.devices.shape
    side = math.isqrt(seq_size)
    grid = jax.sharding.Mesh(
        mesh.devices.reshape(side, seq_size // side, head_size // 2, 2), ("y", "x", "z", "c")
    )
    return jax.shard_map(
        local,
        mesh=grid,
        in_specs=(
            P(SEQ, HEAD),
            P(SEQ, None),
            P(SEQ, None),
            P(SEQ, HEAD),
            P(),
            P(),
            P(),
        ),
        out_specs=(P(SEQ, HEAD), P(HEAD, None, None), P(SEQ, HEAD)),
        check_vma=False,
    )
```
